256 devices in a mesh: dp: 8 (over y, core), seq: 32 (over x, z).
Axes of the slice: x: 4, y: 4, z: 8, core: 2. Of those that a mesh axis runs over, the one named last changes fastest.
Arguments:
- queries: bfloat16 [16, 2048, 1536], P('dp', 'seq'), may hold values from -6 to 6
- key_rows: bfloat16 [16, 2048, 1536], P('dp', 'seq'), may hold values from -6 to 6
- value_rows: bfloat16 [16, 2048, 1536], P('dp', 'seq'), may hold values from -6 to 6
- layer_input: bfloat16 [16, 2048, 1536], P('dp', 'seq'), may hold values from -6 to 6
- utt_lengths: int32 [16], P('dp'), may hold values from 512 to 2048, as said below
- out_weight: bfloat16 [1536, 1536], replicated, may hold values from -0.15625 to 0.15625
- conv_kernel: bfloat16 [31, 1536], replicated, may hold values from -1 to 1
- conv_cotangent: bfloat16 [16, 2048, 1536], P('dp', 'seq'), may hold values from -6 to 6
- pick_weight: int32 [23592], replicated, may hold values from 0 to 2359295
- pick_kernel: int32 [476], replicated, may hold values from 0 to 47615
Outputs:
- conv_out: bfloat16 [16, 2048, 1536], P('dp', 'seq')
- context_grad: bfloat16 [16, 2048, 1536], P('dp', 'seq')
- weight_picks: float32 [23592], replicated
- kernel_picks: float32 [476], replicated
The draws below stay inside these ranges and needn't reach their ends.
Inputs may be any that keep to these rules, and one draw needn't show every extreme that they name: `utt_lengths`: the first utterance fills all 2048 slots and the last has 512 valid frames.
All inputs are finite; a program needn't handle non-finite values.
Results may differ from the reference program's by a relative error of at most 0.0056.
Values may be sent and summed in bfloat16 or wider, within the bound.
No kernel may reach another device: no remote copies, remote signals or barrier semaphores. Data moves between devices by JAX's collectives and lax.ppermute only.
A program may use at most 128 MiB of HBM per device.

```python
import math
import jax
import jax.numpy as jnp
from jax import lax

D = 1536
HEADS = 16
KW = 31
K_WO = 23592
K_KERN = 476
BATCH = 16
FRAMES = 2048


def draw_queries(key, part):
    base = jnp.clip(jax.random.normal(jax.random.fold_in(key, 11), (BATCH, FRAMES, D), jnp.float32), -6.0, 6.0)
    return base.astype(jnp.bfloat16)


def draw_key_rows(key, part):
    base = jnp.clip(jax.random.normal(jax.random.fold_in(key, 13), (BATCH, FRAMES, D), jnp.float32), -6.0, 6.0)
    return base.astype(jnp.bfloat16)


def draw_utt_lengths(key, part):
    drawn = jax.random.randint(jax.random.fold_in(key, 17), (BATCH,), FRAMES // 4, FRAMES + 1, jnp.int32)
    drawn = drawn.at[0].set(FRAMES)
    drawn = drawn.at[BATCH - 1].set(FRAMES // 4)
    return drawn


def place_ends(values, rng, least, high):
    longest = values.shape.index(max(values.shape))
    spots = []
    for shift in (0, 1):
        where = [jax.random.randint(jax.random.fold_in(rng, axis), (), 0, length) for axis, length in enumerate(values.shape)]
        where[longest] = (where[longest] + shift) % values.shape[longest]
        spots.append(tuple(where))
    return values.at[spots[0]].set(least).at[spots[1]].set(high)


def block_scale(key, dims, shards, least, largest):
    def one(dim, shards_of):
        heights = jax.random.uniform(jax.random.fold_in(jax.random.fold_in(key, 6), dim), (shards_of,), jnp.float32, least / len(shards), largest / len(shards))
        return jnp.repeat(jnp.exp(heights), dims[dim] // shards_of).reshape((-1,) + (1,) * (len(dims) - dim - 1))

    factor_of = one(*shards[0])
    for cut in shards[1:]:
        factor_of = factor_of * one(*cut)
    return factor_of


def normal_values(key, extent, spread, limit, cuts=(), kind=jnp.bfloat16):
    level = block_scale(key, extent, cuts, -0.22, 0.18) if cuts else 1.0
    entries = jax.random.normal(key, extent, jnp.float32) * spread * level
    return jnp.minimum(jnp.maximum(entries, -limit), limit).astype(kind)


def setup_inputs(seed: int = 0) -> dict:
    splits = jax.random.split(jax.random.key(seed), 11)
    return {
        "queries": draw_queries(jax.random.fold_in(splits[10], 71), 0),
        "key_rows": draw_key_rows(jax.random.fold_in(splits[10], 71), 0),
        "value_rows": normal_values(splits[2], (BATCH, FRAMES, D), 1.0, 6.0, ((0, 8), (1, 32))),
        "layer_input": normal_values(splits[3], (BATCH, FRAMES, D), 1.0, 6.0, ((0, 8), (1, 32))),
        "utt_lengths": draw_utt_lengths(jax.random.fold_in(splits[10], 71), 0),
        "out_weight": normal_values(splits[5], (D, D), D ** -0.5, 0.15625),
        "conv_kernel": normal_values(splits[6], (KW, D), KW ** -0.5, 1.0),
        "conv_cotangent": normal_values(splits[7], (BATCH, FRAMES, D), 1.0, 6.0, ((0, 8), (1, 32))),
        "pick_weight": place_ends(jax.random.randint(splits[8], (K_WO,), 0, D * D), jax.random.fold_in(splits[8], 1), 0, (D * D) - 1).astype(jnp.int32),
        "pick_kernel": place_ends(jax.random.randint(splits[9], (K_KERN,), 0, KW * D), jax.random.fold_in(splits[9], 1), 0, (KW * D) - 1).astype(jnp.int32),
    }


neg_big = -1e+30

def reference(queries, key_rows, value_rows, layer_input, utt_lengths, out_weight, conv_kernel, conv_cotangent, pick_weight, pick_kernel):
    head_size = D // HEADS
    score_scale = 1.0 / math.sqrt(head_size)
    frame_ids = jnp.arange(FRAMES, dtype=jnp.int32)
    valid_rows = (frame_ids[None, :] < utt_lengths[:, None]).astype(jnp.float32)

    def split_heads(array):
        return array.reshape(BATCH, FRAMES, HEADS, head_size).transpose(0, 2, 1, 3).reshape(BATCH * HEADS, FRAMES, head_size)
    item_lengths = jnp.repeat(utt_lengths, HEADS)

    def one_item(item):
        query_item, key_item, value_item, length_item = item
        scores = jnp.dot(query_item, key_item.T, preferred_element_type=jnp.float32) * score_scale
        scores = jnp.where((frame_ids < length_item)[None, :], scores, neg_big)
        row_max = lax.optimization_barrier(jnp.max(scores, axis=-1, keepdims=True))
        probs = jnp.exp(scores - row_max)
        weights = probs.astype(jnp.bfloat16)
        denom = lax.optimization_barrier(jnp.sum(probs, axis=-1))
        out_rows = jnp.dot(weights, value_item, preferred_element_type=jnp.float32) / denom[:, None]
        return out_rows.astype(jnp.bfloat16)
    context = lax.map(one_item, (split_heads(queries), split_heads(key_rows), split_heads(value_rows), item_lengths))
    context = context.reshape(BATCH, HEADS, FRAMES, head_size).transpose(0, 2, 1, 3).reshape(BATCH, FRAMES, D)
    context_flat = context.reshape(BATCH * FRAMES, D)
    projected = jnp.dot(context_flat, out_weight, preferred_element_type=jnp.float32).reshape(BATCH, FRAMES, D)
    hidden = ((layer_input.astype(jnp.float32) + projected) * valid_rows[:, :, None]).astype(jnp.bfloat16)
    half_taps = (KW - 1) // 2
    kernel_f = conv_kernel.astype(jnp.float32)
    hidden_pad = jnp.pad(hidden.astype(jnp.float32), ((0, 0), (half_taps, half_taps), (0, 0)))
    cot_f = conv_cotangent.astype(jnp.float32)
    conv_sum = jnp.zeros((BATCH, FRAMES, D), jnp.float32)
    kernel_rows = []
    for offset in range(KW):
        window = hidden_pad[:, offset:offset + FRAMES]
        conv_sum = conv_sum + kernel_f[offset] * window
        kernel_rows.append(lax.optimization_barrier(jnp.sum(window * cot_f, axis=(0, 1))))
    conv_out = conv_sum.astype(jnp.bfloat16)
    kernel_grad = jnp.stack(kernel_rows)
    cot_pad = jnp.pad(cot_f, ((0, 0), (2 * half_taps, 2 * half_taps), (0, 0)))
    back_sum = jnp.zeros((BATCH, FRAMES, D), jnp.float32)
    for offset in range(KW):
        begin = 3 * half_taps - offset
        back_sum = back_sum + kernel_f[offset] * cot_pad[:, begin:begin + FRAMES]
    hidden_grad = (back_sum * valid_rows[:, :, None]).astype(jnp.bfloat16)
    grad_flat = hidden_grad.reshape(BATCH * FRAMES, D)
    weight_grad = lax.dot_general(context_flat, grad_flat, (((0,), (0,)), ((), ())), preferred_element_type=jnp.float32)
    context_grad = lax.dot_general(grad_flat, out_weight, (((1,), (1,)), ((), ())), preferred_element_type=jnp.float32)
    context_grad = context_grad.reshape(BATCH, FRAMES, D).astype(jnp.bfloat16)
    norm_factor = 1.0 / math.sqrt(BATCH * FRAMES)
    weight_picks = weight_grad.reshape(-1)[pick_weight] * norm_factor
    kernel_picks = kernel_grad.reshape(-1)[pick_kernel] * norm_factor
    return (conv_out, context_grad, weight_picks, kernel_picks)
```

```python
import math

import jax
import jax.numpy as jnp
from jax import lax
from jax.sharding import PartitionSpec as P

HEADS = 16


neg_big = -1e30


def padded(value, sides, width):
    for axis, dim in sides:
        count, length = (lax.axis_size(axis), value.shape[dim])
        up = [(i, (i + 1) % count) for i in range(count - 1)]
        down = [(j, i) for i, j in up]
        last = lax.slice_in_dim(value, length - width, length, axis=dim)
        leading = lax.slice_in_dim(value, 0, width, axis=dim)
        before = lax.ppermute(last, axis, up)
        after = lax.ppermute(leading, axis, down)
        value = jnp.concatenate([before, value, after], axis=dim)
    return value


def softmax_rows(scores, key_ok):
    scores = jnp.where(key_ok, scores, neg_big)
    row_max = jnp.max(scores, axis=-1, keepdims=True)
    probs = jnp.exp(scores - row_max)
    return (probs.astype(jnp.bfloat16), jnp.sum(probs, axis=-1))


def pick_entries(table, picks):
    flat = table.reshape(-1)
    lane = math.gcd(flat.shape[0], 128)
    blocks = flat.reshape(flat.shape[0] // lane, lane)
    chosen = jnp.take(blocks, picks // lane, axis=0)
    lane_ids = jnp.arange(lane, dtype=jnp.int32)
    hit = lane_ids[None, :] == (picks % lane)[:, None]
    return jnp.sum(jnp.where(hit, chosen, jnp.float32(0.0)), axis=1)


def butterfly_sum(value, axes):
    for axis in axes:
        count = lax.axis_size(axis)
        step = 1
        while step < count:
            pairs = [(i, i ^ step) for i in range(count)]
            value = value + lax.ppermute(value, axis, pairs)
            step *= 2
    return value


def attend(query, key, value, key_ok, score_scale):
    scores = jnp.dot(query, key.T, preferred_element_type=jnp.float32) * score_scale
    weights, denom = softmax_rows(scores, key_ok[None, :])
    out_rows = jnp.dot(weights, value, preferred_element_type=jnp.float32)
    return (out_rows / denom[:, None]).astype(jnp.bfloat16)


def head_attention(queries, key_rows, value_rows, utt_lengths, seq_index, score_scale):
    local_utts, frames_dev, width = queries.shape
    head_size = width // HEADS
    seq_count = HEADS * local_utts
    full_frames = frames_dev * seq_count
    stacked = jnp.stack([queries, key_rows, value_rows])
    stacked = stacked.reshape(3, local_utts, frames_dev, HEADS, head_size)
    stacked = stacked.transpose(3, 1, 0, 2, 4).reshape(seq_count, 3, frames_dev, head_size)
    gathered = lax.all_to_all(stacked, "seq", 0, 0, tiled=True)
    gathered = gathered.transpose(1, 0, 2, 3).reshape(3, full_frames, head_size)
    length = utt_lengths[seq_index % local_utts]
    key_ok = jnp.arange(full_frames, dtype=jnp.int32) < length
    out_rows = attend(gathered[0], gathered[1], gathered[2], key_ok, score_scale)
    out_rows = out_rows.reshape(seq_count, frames_dev, head_size)
    back = lax.all_to_all(out_rows, "seq", 0, 0, tiled=True)
    back = back.reshape(HEADS, local_utts, frames_dev, head_size).transpose(1, 2, 0, 3)
    return back.reshape(local_utts, frames_dev, width)


def frame_attention(queries, key_rows, value_rows, utt_lengths, score_scale):
    local_utts, frames_dev, width = queries.shape
    head_size = width // HEADS
    all_keys = lax.all_gather(key_rows, "seq", axis=1, tiled=True)
    all_values = lax.all_gather(value_rows, "seq", axis=1, tiled=True)
    full_frames = all_keys.shape[1]
    full_ids = jnp.arange(full_frames, dtype=jnp.int32)

    def one_utt(item):
        query_utt, key_utt, value_utt, length_utt = item
        query_heads = query_utt.reshape(frames_dev, HEADS, head_size)
        key_heads = key_utt.reshape(full_frames, HEADS, head_size)
        value_heads = value_utt.reshape(full_frames, HEADS, head_size)
        scores = (
            jnp.einsum("qhd,khd->hqk", query_heads, key_heads, preferred_element_type=jnp.float32)
            * score_scale
        )
        weights, denom = softmax_rows(scores, (full_ids < length_utt)[None, None, :])
        out_rows = jnp.einsum(
            "hqk,khd->qhd", weights, value_heads, preferred_element_type=jnp.float32
        )
        out_rows = out_rows / denom.transpose(1, 0)[:, :, None]
        return out_rows.astype(jnp.bfloat16).reshape(frames_dev, width)

    return lax.map(one_utt, (queries, all_keys, all_values, utt_lengths))


def on_device(
    queries,
    key_rows,
    value_rows,
    layer_input,
    utt_lengths,
    out_weight,
    conv_kernel,
    conv_cotangent,
    pick_weight,
    pick_kernel,
):
    local_utts, frames_dev, width = queries.shape
    seq_count = lax.axis_size("seq")
    full_frames = frames_dev * seq_count
    head_size = width // HEADS
    score_scale = 1.0 / math.sqrt(head_size)
    first_frame = lax.axis_index("seq") * frames_dev
    local_ids = first_frame + jnp.arange(frames_dev, dtype=jnp.int32)
    valid_rows = (local_ids[None, :] < utt_lengths[:, None]).astype(jnp.float32)
    seq_index = lax.axis_index("seq")
    if HEADS * local_utts == seq_count:
        context = head_attention(queries, key_rows, value_rows, utt_lengths, seq_index, score_scale)
    else:
        context = frame_attention(queries, key_rows, value_rows, utt_lengths, score_scale)
    context_flat = context.reshape(local_utts * frames_dev, width)
    projected = jnp.dot(context_flat, out_weight, preferred_element_type=jnp.float32).reshape(
        local_utts, frames_dev, width
    )
    hidden = ((layer_input.astype(jnp.float32) + projected) * valid_rows[:, :, None]).astype(
        jnp.bfloat16
    )
    tap_count = conv_kernel.shape[0]
    half_taps = (tap_count - 1) // 2
    kernel_f = conv_kernel.astype(jnp.float32)
    hidden_pad = padded(hidden, (("seq", 1),), half_taps)
    cot_f = conv_cotangent.astype(jnp.float32)
    conv_sum = jnp.zeros((local_utts, frames_dev, width), jnp.float32)
    kernel_rows = []
    for offset in range(tap_count):
        window = hidden_pad[:, offset : offset + frames_dev].astype(jnp.float32)
        conv_sum = conv_sum + kernel_f[offset] * window
        kernel_rows.append(jnp.sum(window * cot_f, axis=(0, 1)))
    conv_out = conv_sum.astype(jnp.bfloat16)
    kernel_grad = jnp.stack(kernel_rows)
    cot_pad = padded(conv_cotangent, (("seq", 1),), half_taps).astype(jnp.float32)
    back_sum = jnp.zeros((local_utts, frames_dev, width), jnp.float32)
    for offset in range(tap_count):
        begin = 2 * half_taps - offset
        back_sum = back_sum + kernel_f[offset] * cot_pad[:, begin : begin + frames_dev]
    hidden_grad = (back_sum * valid_rows[:, :, None]).astype(jnp.bfloat16)
    grad_flat = hidden_grad.reshape(local_utts * frames_dev, width)
    weight_grad = lax.dot_general(
        context_flat, grad_flat, (((0,), (0,)), ((), ())), preferred_element_type=jnp.float32
    )
    context_grad = lax.dot_general(
        grad_flat, out_weight, (((1,), (1,)), ((), ())), preferred_element_type=jnp.float32
    )
    context_grad = context_grad.reshape(local_utts, frames_dev, width).astype(jnp.bfloat16)
    weight_vals = pick_entries(weight_grad, pick_weight)
    kernel_vals = pick_entries(kernel_grad, pick_kernel)
    joined = butterfly_sum(jnp.concatenate([weight_vals, kernel_vals]), ("dp", "seq"))
    weight_sum, kernel_sum = joined[: weight_vals.shape[0]], joined[weight_vals.shape[0] :]
    total_slots = local_utts * lax.axis_size("dp") * full_frames
    norm_factor = 1.0 / math.sqrt(total_slots)
    return (conv_out, context_grad, weight_sum * norm_factor, kernel_sum * norm_factor)


def solution(mesh):
    placed = (
        P("dp", "seq", None),
        P("dp", "seq", None),
        P("dp", "seq", None),
        P("dp", "seq", None),
        P("dp"),
        P(),
        P(),
        P("dp", "seq", None),
        P(),
        P(),
    )
    return jax.shard_map(
        on_device,
        mesh=mesh,
        in_specs=placed,
        out_specs=(P("dp", "seq", None), P("dp", "seq", None), P(), P()),
        check_vma=False,
    )
```

```python
import math

import jax
import jax.numpy as jnp
from jax import lax
from jax.sharding import PartitionSpec as P

HEADS = 16


neg_big = -1e30


def padded(value, sides, width):
    for axis, dim in sides:
        count, length = (lax.axis_size(axis), value.shape[dim])
        up = [(i, (i + 1) % count) for i in range(count - 1)]
        down = [(j, i) for i, j in up]
        last = lax.slice_in_dim(value, length - width, length, axis=dim)
        leading = lax.slice_in_dim(value, 0, width, axis=dim)
        before = lax.ppermute(last, axis, up)
        after = lax.ppermute(leading, axis, down)
        value = jnp.concatenate([before, value, after], axis=dim)
    return value


def softmax_rows(scores, key_ok):
    scores = jnp.where(key_ok, scores, neg_big)
    row_max = jnp.max(scores, axis=-1, keepdims=True)
    probs = jnp.exp(scores - row_max)
    return (probs.astype(jnp.bfloat16), jnp.sum(probs, axis=-1))


def pick_entries(table, picks):
    flat = table.reshape(-1)
    lane = math.gcd(flat.shape[0], 128)
    blocks = flat.reshape(flat.shape[0] // lane, lane)
    chosen = jnp.take(blocks, picks // lane, axis=0)
    lane_ids = jnp.arange(lane, dtype=jnp.int32)
    hit = lane_ids[None, :] == (picks % lane)[:, None]
    return jnp.sum(jnp.where(hit, chosen, jnp.float32(0.0)), axis=1)


def group_picks(context_flat, grad_flat, picks, axis, levels):
    count = lax.axis_size(axis)
    levels = min(levels, count.bit_length() - 1)
    group = 1 << levels
    pair = jnp.stack([context_flat, grad_flat])
    for level in range(levels):
        step = 1 << level
        other = lax.ppermute(pair, axis, [(i, i ^ step) for i in range(count)])
        pair = jnp.concatenate([pair, other], axis=1)
    table = lax.dot_general(
        pair[0], pair[1], (((0,), (0,)), ((), ())), preferred_element_type=jnp.float32
    )
    total = picks.shape[0]
    rows = -(-total // group)
    padded_picks = jnp.pad(picks, (0, rows * group - total)).reshape(rows, group)
    member = lax.axis_index(axis) % group
    mine = lax.dynamic_index_in_dim(padded_picks, member, axis=1, keepdims=False)
    values = pick_entries(table, mine)
    spread = jnp.where(jnp.arange(group)[None, :] == member, values[:, None], jnp.float32(0.0))
    return spread.reshape(-1)[:total]


def butterfly_sum(value, axes):
    for axis in axes:
        count = lax.axis_size(axis)
        step = 1
        while step < count:
            pairs = [(i, i ^ step) for i in range(count)]
            value = value + lax.ppermute(value, axis, pairs)
            step *= 2
    return value


def attend(query, key, value, key_ok, score_scale):
    scores = jnp.dot(query, key.T, preferred_element_type=jnp.float32) * score_scale
    weights, denom = softmax_rows(scores, key_ok[None, :])
    out_rows = jnp.dot(weights, value, preferred_element_type=jnp.float32)
    return (out_rows / denom[:, None]).astype(jnp.bfloat16)


def head_attention(queries, key_rows, value_rows, utt_lengths, seq_index, score_scale):
    local_utts, frames_dev, width = queries.shape
    head_size = width // HEADS
    seq_count = HEADS * local_utts
    full_frames = frames_dev * seq_count
    stacked = jnp.stack([queries, key_rows, value_rows])
    stacked = stacked.reshape(3, local_utts, frames_dev, HEADS, head_size)
    stacked = stacked.transpose(3, 1, 0, 2, 4).reshape(seq_count, 3, frames_dev, head_size)
    gathered = lax.all_to_all(stacked, "seq", 0, 0, tiled=True)
    gathered = gathered.transpose(1, 0, 2, 3).reshape(3, full_frames, head_size)
    length = utt_lengths[seq_index % local_utts]
    key_ok = jnp.arange(full_frames, dtype=jnp.int32) < length
    out_rows = attend(gathered[0], gathered[1], gathered[2], key_ok, score_scale)
    out_rows = out_rows.reshape(seq_count, frames_dev, head_size)
    back = lax.all_to_all(out_rows, "seq", 0, 0, tiled=True)
    back = back.reshape(HEADS, local_utts, frames_dev, head_size).transpose(1, 2, 0, 3)
    return back.reshape(local_utts, frames_dev, width)


def frame_attention(queries, key_rows, value_rows, utt_lengths, score_scale):
    local_utts, frames_dev, width = queries.shape
    head_size = width // HEADS
    all_keys = lax.all_gather(key_rows, "seq", axis=1, tiled=True)
    all_values = lax.all_gather(value_rows, "seq", axis=1, tiled=True)
    full_frames = all_keys.shape[1]
    full_ids = jnp.arange(full_frames, dtype=jnp.int32)

    def one_utt(item):
        query_utt, key_utt, value_utt, length_utt = item
        query_heads = query_utt.reshape(frames_dev, HEADS, head_size)
        key_heads = key_utt.reshape(full_frames, HEADS, head_size)
        value_heads = value_utt.reshape(full_frames, HEADS, head_size)
        scores = (
            jnp.einsum("qhd,khd->hqk", query_heads, key_heads, preferred_element_type=jnp.float32)
            * score_scale
        )
        weights, denom = softmax_rows(scores, (full_ids < length_utt)[None, None, :])
        out_rows = jnp.einsum(
            "hqk,khd->qhd", weights, value_heads, preferred_element_type=jnp.float32
        )
        out_rows = out_rows / denom.transpose(1, 0)[:, :, None]
        return out_rows.astype(jnp.bfloat16).reshape(frames_dev, width)

    return lax.map(one_utt, (queries, all_keys, all_values, utt_lengths))


def on_device(
    queries,
    key_rows,
    value_rows,
    layer_input,
    utt_lengths,
    out_weight,
    conv_kernel,
    conv_cotangent,
    pick_weight,
    pick_kernel,
):
    local_utts, frames_dev, width = queries.shape
    seq_count = lax.axis_size("seq")
    full_frames = frames_dev * seq_count
    head_size = width // HEADS
    score_scale = 1.0 / math.sqrt(head_size)
    first_frame = lax.axis_index("seq") * frames_dev
    local_ids = first_frame + jnp.arange(frames_dev, dtype=jnp.int32)
    valid_rows = (local_ids[None, :] < utt_lengths[:, None]).astype(jnp.float32)
    seq_index = lax.axis_index("seq")
    if HEADS * local_utts == seq_count:
        context = head_attention(queries, key_rows, value_rows, utt_lengths, seq_index, score_scale)
    else:
        context = frame_attention(queries, key_rows, value_rows, utt_lengths, score_scale)
    context_flat = context.reshape(local_utts * frames_dev, width)
    projected = jnp.dot(context_flat, out_weight, preferred_element_type=jnp.float32).reshape(
        local_utts, frames_dev, width
    )
    hidden = ((layer_input.astype(jnp.float32) + projected) * valid_rows[:, :, None]).astype(
        jnp.bfloat16
    )
    tap_count = conv_kernel.shape[0]
    half_taps = (tap_count - 1) // 2
    kernel_f = conv_kernel.astype(jnp.float32)
    hidden_pad = padded(hidden, (("seq", 1),), half_taps)
    cot_f = conv_cotangent.astype(jnp.float32)
    conv_sum = jnp.zeros((local_utts, frames_dev, width), jnp.float32)
    kernel_rows = []
    for offset in range(tap_count):
        window = hidden_pad[:, offset : offset + frames_dev].astype(jnp.float32)
        conv_sum = conv_sum + kernel_f[offset] * window
        kernel_rows.append(jnp.sum(window * cot_f, axis=(0, 1)))
    conv_out = conv_sum.astype(jnp.bfloat16)
    kernel_grad = jnp.stack(kernel_rows)
    cot_pad = padded(conv_cotangent, (("seq", 1),), half_taps).astype(jnp.float32)
    back_sum = jnp.zeros((local_utts, frames_dev, width), jnp.float32)
    for offset in range(tap_count):
        begin = 2 * half_taps - offset
        back_sum = back_sum + kernel_f[offset] * cot_pad[:, begin : begin + frames_dev]
    hidden_grad = (back_sum * valid_rows[:, :, None]).astype(jnp.bfloat16)
    grad_flat = hidden_grad.reshape(local_utts * frames_dev, width)
    context_grad = lax.dot_general(
        grad_flat, out_weight, (((1,), (1,)), ((), ())), preferred_element_type=jnp.float32
    )
    context_grad = context_grad.reshape(local_utts, frames_dev, width).astype(jnp.bfloat16)
    weight_vals = group_picks(context_flat, grad_flat, pick_weight, "dp", 2)
    kernel_vals = pick_entries(kernel_grad, pick_kernel)
    joined = butterfly_sum(jnp.concatenate([weight_vals, kernel_vals]), ("dp", "seq"))
    weight_sum, kernel_sum = joined[: weight_vals.shape[0]], joined[weight_vals.shape[0] :]
    total_slots = local_utts * lax.axis_size("dp") * full_frames
    norm_factor = 1.0 / math.sqrt(total_slots)
    return (conv_out, context_grad, weight_sum * norm_factor, kernel_sum * norm_factor)


def solution(mesh):
    placed = (
        P("dp", "seq", None),
        P("dp", "seq", None),
        P("dp", "seq", None),
        P("dp", "seq", None),
        P("dp"),
        P(),
        P(),
        P("dp", "seq", None),
        P(),
        P(),
    )
    return jax.shard_map(
        on_device,
        mesh=mesh,
        in_specs=placed,
        out_specs=(P("dp", "seq", None), P("dp", "seq", None), P(), P()),
        check_vma=False,
    )
```

```python
import math

import jax
import jax.numpy as jnp
from jax import lax
from jax.sharding import PartitionSpec as P

HEADS = 16


neg_big = -1e30


def padded(value, sides, width):
    for axis, dim in sides:
        count, length = (lax.axis_size(axis), value.shape[dim])
        up = [(i, (i + 1) % count) for i in range(count - 1)]
        down = [(j, i) for i, j in up]
        last = lax.slice_in_dim(value, length - width, length, axis=dim)
        leading = lax.slice_in_dim(value, 0, width, axis=dim)
        before = lax.ppermute(last, axis, up)
        after = lax.ppermute(leading, axis, down)
        value = jnp.concatenate([before, value, after], axis=dim)
    return value


def softmax_rows(scores, key_ok):
    scores = jnp.where(key_ok, scores, neg_big)
    row_max = jnp.max(scores, axis=-1, keepdims=True)
    probs = jnp.exp(scores - row_max)
    return (probs.astype(jnp.bfloat16), jnp.sum(probs, axis=-1))


def pick_entries(table, picks):
    flat = table.reshape(-1)
    lane = math.gcd(flat.shape[0], 128)
    blocks = flat.reshape(flat.shape[0] // lane, lane)
    chosen = jnp.take(blocks, picks // lane, axis=0)
    lane_ids = jnp.arange(lane, dtype=jnp.int32)
    hit = lane_ids[None, :] == (picks % lane)[:, None]
    return jnp.sum(jnp.where(hit, chosen, jnp.float32(0.0)), axis=1)

def group_picks(context_flat, grad_flat, picks, axis, levels):
    count = lax.axis_size(axis)
    levels = min(levels, count.bit_length() - 1)
    group = 1 << levels
    pair = jnp.stack([context_flat, grad_flat])
    for level in range(levels):
        step = 1 << level
        other = lax.ppermute(pair, axis, [(i, i ^ step) for i in range(count)])
        pair = jnp.concatenate([pair, other], axis=1)
    table = lax.dot_general(
        pair[0], pair[1], (((0,), (0,)), ((), ())), preferred_element_type=jnp.float32
    )
    total = picks.shape[0]
    rows = -(-total // group)
    padded_picks = jnp.pad(picks, (0, rows * group - total)).reshape(rows, group)
    member = lax.axis_index(axis) % group
    mine = lax.dynamic_index_in_dim(padded_picks, member, axis=1, keepdims=False)
    values = pick_entries(table, mine)
    spread = jnp.where(jnp.arange(group)[None, :] == member, values[:, None], jnp.float32(0.0))
    return spread.reshape(-1)[:total]


def butterfly_sum(value, axes):
    for axis in axes:
        count = lax.axis_size(axis)
        step = 1
        while step < count:
            pairs = [(i, i ^ step) for i in range(count)]
            value = value + lax.ppermute(value, axis, pairs)
            step *= 2
    return value


def attend(query, key, value, key_ok, score_scale):
    scores = jnp.dot(query, key.T, preferred_element_type=jnp.float32) * score_scale
    weights, denom = softmax_rows(scores, key_ok[None, :])
    out_rows = jnp.dot(weights, value, preferred_element_type=jnp.float32)
    return (out_rows / denom[:, None]).astype(jnp.bfloat16)


def head_attention(queries, key_rows, value_rows, utt_lengths, seq_index, score_scale, later):
    local_utts, frames_dev, width = queries.shape
    head_size = width // HEADS
    seq_count = HEADS * local_utts
    full_frames = frames_dev * seq_count
    stacked = jnp.stack([queries, key_rows, value_rows])
    stacked = stacked.reshape(3, local_utts, frames_dev, HEADS, head_size)
    stacked = stacked.transpose(3, 1, 0, 2, 4).reshape(seq_count, 3, frames_dev, head_size)
    gathered = lax.all_to_all(stacked, "seq", 0, 0, tiled=True)
    gathered, later = lax.optimization_barrier((gathered, later))
    gathered = gathered.transpose(1, 0, 2, 3).reshape(3, full_frames, head_size)
    length = utt_lengths[seq_index % local_utts]
    key_ok = jnp.arange(full_frames, dtype=jnp.int32) < length
    out_rows = attend(gathered[0], gathered[1], gathered[2], key_ok, score_scale)
    out_rows = out_rows.reshape(seq_count, frames_dev, head_size)
    back = lax.all_to_all(out_rows, "seq", 0, 0, tiled=True)
    back = back.reshape(HEADS, local_utts, frames_dev, head_size).transpose(1, 2, 0, 3)
    return back.reshape(local_utts, frames_dev, width), later


def frame_attention(queries, key_rows, value_rows, utt_lengths, score_scale):
    local_utts, frames_dev, width = queries.shape
    head_size = width // HEADS
    all_keys = lax.all_gather(key_rows, "seq", axis=1, tiled=True)
    all_values = lax.all_gather(value_rows, "seq", axis=1, tiled=True)
    full_frames = all_keys.shape[1]
    full_ids = jnp.arange(full_frames, dtype=jnp.int32)

    def one_utt(item):
        query_utt, key_utt, value_utt, length_utt = item
        query_heads = query_utt.reshape(frames_dev, HEADS, head_size)
        key_heads = key_utt.reshape(full_frames, HEADS, head_size)
        value_heads = value_utt.reshape(full_frames, HEADS, head_size)
        scores = (
            jnp.einsum("qhd,khd->hqk", query_heads, key_heads, preferred_element_type=jnp.float32)
            * score_scale
        )
        weights, denom = softmax_rows(scores, (full_ids < length_utt)[None, None, :])
        out_rows = jnp.einsum(
            "hqk,khd->qhd", weights, value_heads, preferred_element_type=jnp.float32
        )
        out_rows = out_rows / denom.transpose(1, 0)[:, :, None]
        return out_rows.astype(jnp.bfloat16).reshape(frames_dev, width)

    return lax.map(one_utt, (queries, all_keys, all_values, utt_lengths))


def on_device(
    queries,
    key_rows,
    value_rows,
    layer_input,
    utt_lengths,
    out_weight,
    conv_kernel,
    conv_cotangent,
    pick_weight,
    pick_kernel,
):
    local_utts, frames_dev, width = queries.shape
    seq_count = lax.axis_size("seq")
    full_frames = frames_dev * seq_count
    head_size = width // HEADS
    score_scale = 1.0 / math.sqrt(head_size)
    first_frame = lax.axis_index("seq") * frames_dev
    local_ids = first_frame + jnp.arange(frames_dev, dtype=jnp.int32)
    valid_rows = (local_ids[None, :] < utt_lengths[:, None]).astype(jnp.float32)
    seq_index = lax.axis_index("seq")
    if HEADS * local_utts == seq_count:
        context, conv_cotangent = head_attention(
            queries, key_rows, value_rows, utt_lengths, seq_index, score_scale, conv_cotangent
        )
    else:
        context = frame_attention(queries, key_rows, value_rows, utt_lengths, score_scale)
    context_flat = context.reshape(local_utts * frames_dev, width)
    projected = jnp.dot(context_flat, out_weight, preferred_element_type=jnp.float32).reshape(
        local_utts, frames_dev, width
    )
    hidden = ((layer_input.astype(jnp.float32) + projected) * valid_rows[:, :, None]).astype(
        jnp.bfloat16
    )
    tap_count = conv_kernel.shape[0]
    half_taps = (tap_count - 1) // 2
    kernel_f = conv_kernel.astype(jnp.float32)
    hidden_pad = padded(hidden, (("seq", 1),), half_taps)
    cot_f = conv_cotangent.astype(jnp.float32)
    conv_sum = jnp.zeros((local_utts, frames_dev, width), jnp.float32)
    kernel_rows = []
    for offset in range(tap_count):
        window = hidden_pad[:, offset : offset + frames_dev].astype(jnp.float32)
        conv_sum = conv_sum + kernel_f[offset] * window
        kernel_rows.append(jnp.sum(window * cot_f, axis=(0, 1)))
    conv_out = conv_sum.astype(jnp.bfloat16)
    kernel_grad = jnp.stack(kernel_rows)
    cot_pad = padded(conv_cotangent, (("seq", 1),), half_taps).astype(jnp.float32)
    back_sum = jnp.zeros((local_utts, frames_dev, width), jnp.float32)
    for offset in range(tap_count):
        begin = 2 * half_taps - offset
        back_sum = back_sum + kernel_f[offset] * cot_pad[:, begin : begin + frames_dev]
    hidden_grad = (back_sum * valid_rows[:, :, None]).astype(jnp.bfloat16)
    grad_flat = hidden_grad.reshape(local_utts * frames_dev, width)
    context_grad = lax.dot_general(
        grad_flat, out_weight, (((1,), (1,)), ((), ())), preferred_element_type=jnp.float32
    )
    context_grad = context_grad.reshape(local_utts, frames_dev, width).astype(jnp.bfloat16)
    weight_vals = group_picks(context_flat, grad_flat, pick_weight, "dp", 1)
    kernel_vals = pick_entries(kernel_grad, pick_kernel)
    joined = butterfly_sum(jnp.concatenate([weight_vals, kernel_vals]), ("dp", "seq"))
    weight_sum, kernel_sum = joined[: weight_vals.shape[0]], joined[weight_vals.shape[0] :]
    total_slots = local_utts * lax.axis_size("dp") * full_frames
    norm_factor = 1.0 / math.sqrt(total_slots)
    return (conv_out, context_grad, weight_sum * norm_factor, kernel_sum * norm_factor)


def solution(mesh):
    placed = (
        P("dp", "seq", None),
        P("dp", "seq", None),
        P("dp", "seq", None),
        P("dp", "seq", None),
        P("dp"),
        P(),
        P(),
        P("dp", "seq", None),
        P(),
        P(),
    )
    return jax.shard_map(
        on_device,
        mesh=mesh,
        in_specs=placed,
        out_specs=(P("dp", "seq", None), P("dp", "seq", None), P(), P()),
        check_vma=False,
    )
```

```python
import math

import jax
import jax.numpy as jnp
from jax import lax
from jax.sharding import PartitionSpec as P

HEADS = 16


neg_big = -1e30


def padded(value, sides, width):
    for axis, dim in sides:
        count, length = (lax.axis_size(axis), value.shape[dim])
        up = [(i, (i + 1) % count) for i in range(count - 1)]
        down = [(j, i) for i, j in up]
        last = lax.slice_in_dim(value, length - width, length, axis=dim)
        leading = lax.slice_in_dim(value, 0, width, axis=dim)
        before = lax.ppermute(last, axis, up)
        after = lax.ppermute(leading, axis, down)
        value = jnp.concatenate([before, value, after], axis=dim)
    return value


def softmax_rows(scores, key_ok):
    scores = jnp.where(key_ok, scores, neg_big)
    row_max = jnp.max(scores, axis=-1, keepdims=True)
    probs = jnp.exp(scores - row_max)
    return (probs.astype(jnp.bfloat16), jnp.sum(probs, axis=-1))


def pick_entries(table, picks):
    flat = table.reshape(-1)
    lane = math.gcd(flat.shape[0], 128)
    blocks = flat.reshape(flat.shape[0] // lane, lane)
    chosen = jnp.take(blocks, picks // lane, axis=0)
    lane_ids = jnp.arange(lane, dtype=jnp.int32)
    hit = lane_ids[None, :] == (picks % lane)[:, None]
    return jnp.sum(jnp.where(hit, chosen, jnp.float32(0.0)), axis=1)

def group_picks(context_flat, grad_flat, picks, axis, levels):
    count = lax.axis_size(axis)
    levels = min(levels, count.bit_length() - 1)
    group = 1 << levels
    pair = jnp.stack([context_flat, grad_flat])
    for level in range(levels):
        step = 1 << level
        other = lax.ppermute(pair, axis, [(i, i ^ step) for i in range(count)])
        pair = jnp.concatenate([pair, other], axis=1)
    table = lax.dot_general(
        pair[0], pair[1], (((0,), (0,)), ((), ())), preferred_element_type=jnp.float32
    )
    total = picks.shape[0]
    rows = -(-total // group)
    padded_picks = jnp.pad(picks, (0, rows * group - total))
    first = (lax.axis_index(axis) % group) * rows
    mine = lax.dynamic_slice(padded_picks, (first,), (rows,))
    values = pick_entries(table, mine)
    spread = lax.dynamic_update_slice(jnp.zeros((rows * group,), jnp.float32), values, (first,))
    return spread[:total]


def butterfly_sum(value, axes):
    for axis in axes:
        count = lax.axis_size(axis)
        step = 1
        while step < count:
            pairs = [(i, i ^ step) for i in range(count)]
            value = value + lax.ppermute(value, axis, pairs)
            step *= 2
    return value


def attend(query, key, value, key_ok, score_scale):
    scores = jnp.dot(query, key.T, preferred_element_type=jnp.float32) * score_scale
    weights, denom = softmax_rows(scores, key_ok[None, :])
    out_rows = jnp.dot(weights, value, preferred_element_type=jnp.float32)
    return (out_rows / denom[:, None]).astype(jnp.bfloat16)


def head_attention(queries, key_rows, value_rows, utt_lengths, seq_index, score_scale, later):
    local_utts, frames_dev, width = queries.shape
    head_size = width // HEADS
    seq_count = HEADS * local_utts
    full_frames = frames_dev * seq_count
    stacked = jnp.stack([queries, key_rows, value_rows])
    stacked = stacked.reshape(3, local_utts, frames_dev, HEADS, head_size)
    stacked = stacked.transpose(3, 1, 0, 2, 4).reshape(seq_count, 3, frames_dev, head_size)
    gathered = lax.all_to_all(stacked, "seq", 0, 0, tiled=True)
    gathered, later = lax.optimization_barrier((gathered, later))
    gathered = gathered.transpose(1, 0, 2, 3).reshape(3, full_frames, head_size)
    length = utt_lengths[seq_index % local_utts]
    key_ok = jnp.arange(full_frames, dtype=jnp.int32) < length
    out_rows = attend(gathered[0], gathered[1], gathered[2], key_ok, score_scale)
    out_rows = out_rows.reshape(seq_count, frames_dev, head_size)
    back = lax.all_to_all(out_rows, "seq", 0, 0, tiled=True)
    back = back.reshape(HEADS, local_utts, frames_dev, head_size).transpose(1, 2, 0, 3)
    return back.reshape(local_utts, frames_dev, width), later


def frame_attention(queries, key_rows, value_rows, utt_lengths, score_scale):
    local_utts, frames_dev, width = queries.shape
    head_size = width // HEADS
    all_keys = lax.all_gather(key_rows, "seq", axis=1, tiled=True)
    all_values = lax.all_gather(value_rows, "seq", axis=1, tiled=True)
    full_frames = all_keys.shape[1]
    full_ids = jnp.arange(full_frames, dtype=jnp.int32)

    def one_utt(item):
        query_utt, key_utt, value_utt, length_utt = item
        query_heads = query_utt.reshape(frames_dev, HEADS, head_size)
        key_heads = key_utt.reshape(full_frames, HEADS, head_size)
        value_heads = value_utt.reshape(full_frames, HEADS, head_size)
        scores = (
            jnp.einsum("qhd,khd->hqk", query_heads, key_heads, preferred_element_type=jnp.float32)
            * score_scale
        )
        weights, denom = softmax_rows(scores, (full_ids < length_utt)[None, None, :])
        out_rows = jnp.einsum(
            "hqk,khd->qhd", weights, value_heads, preferred_element_type=jnp.float32
        )
        out_rows = out_rows / denom.transpose(1, 0)[:, :, None]
        return out_rows.astype(jnp.bfloat16).reshape(frames_dev, width)

    return lax.map(one_utt, (queries, all_keys, all_values, utt_lengths))


def on_device(
    queries,
    key_rows,
    value_rows,
    layer_input,
    utt_lengths,
    out_weight,
    conv_kernel,
    conv_cotangent,
    pick_weight,
    pick_kernel,
):
    local_utts, frames_dev, width = queries.shape
    seq_count = lax.axis_size("seq")
    full_frames = frames_dev * seq_count
    head_size = width // HEADS
    score_scale = 1.0 / math.sqrt(head_size)
    first_frame = lax.axis_index("seq") * frames_dev
    local_ids = first_frame + jnp.arange(frames_dev, dtype=jnp.int32)
    valid_rows = (local_ids[None, :] < utt_lengths[:, None]).astype(jnp.float32)
    seq_index = lax.axis_index("seq")
    if HEADS * local_utts == seq_count:
        context, conv_cotangent = head_attention(
            queries, key_rows, value_rows, utt_lengths, seq_index, score_scale, conv_cotangent
        )
    else:
        context = frame_attention(queries, key_rows, value_rows, utt_lengths, score_scale)
    context_flat = context.reshape(local_utts * frames_dev, width)
    projected = jnp.dot(context_flat, out_weight, preferred_element_type=jnp.float32).reshape(
        local_utts, frames_dev, width
    )
    hidden = ((layer_input.astype(jnp.float32) + projected) * valid_rows[:, :, None]).astype(
        jnp.bfloat16
    )
    tap_count = conv_kernel.shape[0]
    half_taps = (tap_count - 1) // 2
    kernel_f = conv_kernel.astype(jnp.float32)
    hidden_pad = padded(hidden, (("seq", 1),), half_taps)
    cot_f = conv_cotangent.astype(jnp.float32)
    conv_sum = jnp.zeros((local_utts, frames_dev, width), jnp.float32)
    kernel_rows = []
    for offset in range(tap_count):
        window = hidden_pad[:, offset : offset + frames_dev].astype(jnp.float32)
        conv_sum = conv_sum + kernel_f[offset] * window
        kernel_rows.append(jnp.sum(window * cot_f, axis=(0, 1)))
    conv_out = conv_sum.astype(jnp.bfloat16)
    kernel_grad = jnp.stack(kernel_rows)
    cot_pad = padded(conv_cotangent, (("seq", 1),), half_taps).astype(jnp.float32)
    back_sum = jnp.zeros((local_utts, frames_dev, width), jnp.float32)
    for offset in range(tap_count):
        begin = 2 * half_taps - offset
        back_sum = back_sum + kernel_f[offset] * cot_pad[:, begin : begin + frames_dev]
    hidden_grad = (back_sum * valid_rows[:, :, None]).astype(jnp.bfloat16)
    grad_flat = hidden_grad.reshape(local_utts * frames_dev, width)
    context_grad = lax.dot_general(
        grad_flat, out_weight, (((1,), (1,)), ((), ())), preferred_element_type=jnp.float32
    )
    context_grad = context_grad.reshape(local_utts, frames_dev, width).astype(jnp.bfloat16)
    weight_vals = group_picks(context_flat, grad_flat, pick_weight, "dp", 1)
    kernel_vals = pick_entries(kernel_grad, pick_kernel)
    joined = butterfly_sum(jnp.concatenate([weight_vals, kernel_vals]), ("dp", "seq"))
    weight_sum, kernel_sum = joined[: weight_vals.shape[0]], joined[weight_vals.shape[0] :]
    total_slots = local_utts * lax.axis_size("dp") * full_frames
    norm_factor = 1.0 / math.sqrt(total_slots)
    return (conv_out, context_grad, weight_sum * norm_factor, kernel_sum * norm_factor)


def solution(mesh):
    placed = (
        P("dp", "seq", None),
        P("dp", "seq", None),
        P("dp", "seq", None),
        P("dp", "seq", None),
        P("dp"),
        P(),
        P(),
        P("dp", "seq", None),
        P(),
        P(),
    )
    return jax.shard_map(
        on_device,
        mesh=mesh,
        in_specs=placed,
        out_specs=(P("dp", "seq", None), P("dp", "seq", None), P(), P()),
        check_vma=False,
    )
```

```python
import math

import jax
import jax.numpy as jnp
from jax import lax
from jax.sharding import PartitionSpec as P

HEADS = 16


neg_big = -1e30


def padded(value, sides, width):
    for axis, dim in sides:
        count, length = (lax.axis_size(axis), value.shape[dim])
        up = [(i, (i + 1) % count) for i in range(count - 1)]
        down = [(j, i) for i, j in up]
        last = lax.slice_in_dim(value, length - width, length, axis=dim)
        leading = lax.slice_in_dim(value, 0, width, axis=dim)
        before = lax.ppermute(last, axis, up)
        after = lax.ppermute(leading, axis, down)
        value = jnp.concatenate([before, value, after], axis=dim)
    return value


def softmax_rows(scores, key_ok):
    scores = jnp.where(key_ok, scores, neg_big)
    row_max = jnp.max(scores, axis=-1, keepdims=True)
    probs = jnp.exp(scores - row_max)
    return (probs.astype(jnp.bfloat16), jnp.sum(probs, axis=-1))


def pick_entries(table, picks):
    flat = table.reshape(-1)
    lane = math.gcd(flat.shape[0], 128)
    blocks = flat.reshape(flat.shape[0] // lane, lane)
    chosen = jnp.take(blocks, picks // lane, axis=0)
    lane_ids = jnp.arange(lane, dtype=jnp.int32)
    hit = lane_ids[None, :] == (picks % lane)[:, None]
    return jnp.sum(jnp.where(hit, chosen, jnp.float32(0.0)), axis=1)

def group_picks(context_flat, grad_flat, picks, axis, levels):
    count = lax.axis_size(axis)
    levels = min(levels, count.bit_length() - 1)
    group = 1 << levels
    pair = jnp.stack([context_flat, grad_flat])
    for level in range(levels):
        step = 1 << level
        other = lax.ppermute(pair, axis, [(i, i ^ step) for i in range(count)])
        pair = jnp.concatenate([pair, other], axis=1)
    table = lax.dot_general(
        pair[0], pair[1], (((0,), (0,)), ((), ())), preferred_element_type=jnp.float32
    )
    total = picks.shape[0]
    rows = -(-total // group)
    padded_picks = jnp.pad(picks, (0, rows * group - total))
    first = (lax.axis_index(axis) % group) * rows
    mine = lax.dynamic_slice(padded_picks, (first,), (rows,))
    values = pick_entries(table, mine)
    spread = lax.dynamic_update_slice(jnp.zeros((rows * group,), jnp.float32), values, (first,))
    return spread[:total]


def butterfly_sum(value, axes, radix_bits=3):
    for axis in axes:
        count = lax.axis_size(axis)
        index = lax.axis_index(axis)
        low = 0
        while (1 << low) < count:
            bits = min(radix_bits, (count - 1).bit_length() - low)
            size = 1 << bits
            member = (index >> low) % size
            parts = [value]
            for t in range(1, size):
                pairs = [(i, i ^ (t << low)) for i in range(count)]
                parts.append(lax.ppermute(value, axis, pairs))
            stacked = jnp.stack(parts)
            total = lax.dynamic_index_in_dim(stacked, member, keepdims=False)
            for j in range(1, size):
                total = total + lax.dynamic_index_in_dim(stacked, member ^ j, keepdims=False)
            value = total
            low += bits
    return value

def attend(query, key, value, key_ok, score_scale):
    scores = jnp.dot(query, key.T, preferred_element_type=jnp.float32) * score_scale
    weights, denom = softmax_rows(scores, key_ok[None, :])
    out_rows = jnp.dot(weights, value, preferred_element_type=jnp.float32)
    return (out_rows / denom[:, None]).astype(jnp.bfloat16)


def head_attention(queries, key_rows, value_rows, utt_lengths, seq_index, score_scale, later):
    local_utts, frames_dev, width = queries.shape
    head_size = width // HEADS
    seq_count = HEADS * local_utts
    full_frames = frames_dev * seq_count
    stacked = jnp.stack([queries, key_rows, value_rows])
    stacked = stacked.reshape(3, local_utts, frames_dev, HEADS, head_size)
    stacked = stacked.transpose(3, 1, 0, 2, 4).reshape(seq_count, 3, frames_dev, head_size)
    gathered = lax.all_to_all(stacked, "seq", 0, 0, tiled=True)
    gathered, later = lax.optimization_barrier((gathered, later))
    gathered = gathered.transpose(1, 0, 2, 3).reshape(3, full_frames, head_size)
    length = utt_lengths[seq_index % local_utts]
    key_ok = jnp.arange(full_frames, dtype=jnp.int32) < length
    out_rows = attend(gathered[0], gathered[1], gathered[2], key_ok, score_scale)
    out_rows = out_rows.reshape(seq_count, frames_dev, head_size)
    back = lax.all_to_all(out_rows, "seq", 0, 0, tiled=True)
    back = back.reshape(HEADS, local_utts, frames_dev, head_size).transpose(1, 2, 0, 3)
    return back.reshape(local_utts, frames_dev, width), later


def frame_attention(queries, key_rows, value_rows, utt_lengths, score_scale):
    local_utts, frames_dev, width = queries.shape
    head_size = width // HEADS
    all_keys = lax.all_gather(key_rows, "seq", axis=1, tiled=True)
    all_values = lax.all_gather(value_rows, "seq", axis=1, tiled=True)
    full_frames = all_keys.shape[1]
    full_ids = jnp.arange(full_frames, dtype=jnp.int32)

    def one_utt(item):
        query_utt, key_utt, value_utt, length_utt = item
        query_heads = query_utt.reshape(frames_dev, HEADS, head_size)
        key_heads = key_utt.reshape(full_frames, HEADS, head_size)
        value_heads = value_utt.reshape(full_frames, HEADS, head_size)
        scores = (
            jnp.einsum("qhd,khd->hqk", query_heads, key_heads, preferred_element_type=jnp.float32)
            * score_scale
        )
        weights, denom = softmax_rows(scores, (full_ids < length_utt)[None, None, :])
        out_rows = jnp.einsum(
            "hqk,khd->qhd", weights, value_heads, preferred_element_type=jnp.float32
        )
        out_rows = out_rows / denom.transpose(1, 0)[:, :, None]
        return out_rows.astype(jnp.bfloat16).reshape(frames_dev, width)

    return lax.map(one_utt, (queries, all_keys, all_values, utt_lengths))


def on_device(
    queries,
    key_rows,
    value_rows,
    layer_input,
    utt_lengths,
    out_weight,
    conv_kernel,
    conv_cotangent,
    pick_weight,
    pick_kernel,
):
    local_utts, frames_dev, width = queries.shape
    seq_count = lax.axis_size("seq")
    full_frames = frames_dev * seq_count
    head_size = width // HEADS
    score_scale = 1.0 / math.sqrt(head_size)
    first_frame = lax.axis_index("seq") * frames_dev
    local_ids = first_frame + jnp.arange(frames_dev, dtype=jnp.int32)
    valid_rows = (local_ids[None, :] < utt_lengths[:, None]).astype(jnp.float32)
    seq_index = lax.axis_index("seq")
    if HEADS * local_utts == seq_count:
        context, conv_cotangent = head_attention(
            queries, key_rows, value_rows, utt_lengths, seq_index, score_scale, conv_cotangent
        )
    else:
        context = frame_attention(queries, key_rows, value_rows, utt_lengths, score_scale)
    context_flat = context.reshape(local_utts * frames_dev, width)
    projected = jnp.dot(context_flat, out_weight, preferred_element_type=jnp.float32).reshape(
        local_utts, frames_dev, width
    )
    hidden = ((layer_input.astype(jnp.float32) + projected) * valid_rows[:, :, None]).astype(
        jnp.bfloat16
    )
    tap_count = conv_kernel.shape[0]
    half_taps = (tap_count - 1) // 2
    kernel_f = conv_kernel.astype(jnp.float32)
    hidden_pad = padded(hidden, (("seq", 1),), half_taps)
    cot_f = conv_cotangent.astype(jnp.float32)
    conv_sum = jnp.zeros((local_utts, frames_dev, width), jnp.float32)
    kernel_rows = []
    for offset in range(tap_count):
        window = hidden_pad[:, offset : offset + frames_dev].astype(jnp.float32)
        conv_sum = conv_sum + kernel_f[offset] * window
        kernel_rows.append(jnp.sum(window * cot_f, axis=(0, 1)))
    conv_out = conv_sum.astype(jnp.bfloat16)
    kernel_grad = jnp.stack(kernel_rows)
    cot_pad = padded(conv_cotangent, (("seq", 1),), half_taps).astype(jnp.float32)
    back_sum = jnp.zeros((local_utts, frames_dev, width), jnp.float32)
    for offset in range(tap_count):
        begin = 2 * half_taps - offset
        back_sum = back_sum + kernel_f[offset] * cot_pad[:, begin : begin + frames_dev]
    hidden_grad = (back_sum * valid_rows[:, :, None]).astype(jnp.bfloat16)
    grad_flat = hidden_grad.reshape(local_utts * frames_dev, width)
    context_grad = lax.dot_general(
        grad_flat, out_weight, (((1,), (1,)), ((), ())), preferred_element_type=jnp.float32
    )
    context_grad = context_grad.reshape(local_utts, frames_dev, width).astype(jnp.bfloat16)
    weight_vals = group_picks(context_flat, grad_flat, pick_weight, "dp", 1)
    kernel_vals = pick_entries(kernel_grad, pick_kernel)
    joined = butterfly_sum(jnp.concatenate([weight_vals, kernel_vals]), ("dp", "seq"))
    weight_sum, kernel_sum = joined[: weight_vals.shape[0]], joined[weight_vals.shape[0] :]
    total_slots = local_utts * lax.axis_size("dp") * full_frames
    norm_factor = 1.0 / math.sqrt(total_slots)
    return (conv_out, context_grad, weight_sum * norm_factor, kernel_sum * norm_factor)


def solution(mesh):
    placed = (
        P("dp", "seq", None),
        P("dp", "seq", None),
        P("dp", "seq", None),
        P("dp", "seq", None),
        P("dp"),
        P(),
        P(),
        P("dp", "seq", None),
        P(),
        P(),
    )
    return jax.shard_map(
        on_device,
        mesh=mesh,
        in_specs=placed,
        out_specs=(P("dp", "seq", None), P("dp", "seq", None), P(), P()),
        check_vma=False,
    )
```

```python
import math

import jax
import jax.numpy as jnp
from jax import lax
from jax.sharding import PartitionSpec as P

HEADS = 16


neg_big = -1e30


def padded(value, sides, width):
    for axis, dim in sides:
        count, length = (lax.axis_size(axis), value.shape[dim])
        up = [(i, (i + 1) % count) for i in range(count - 1)]
        down = [(j, i) for i, j in up]
        last = lax.slice_in_dim(value, length - width, length, axis=dim)
        leading = lax.slice_in_dim(value, 0, width, axis=dim)
        before = lax.ppermute(last, axis, up)
        after = lax.ppermute(leading, axis, down)
        value = jnp.concatenate([before, value, after], axis=dim)
    return value


def softmax_rows(scores, key_ok):
    scores = jnp.where(key_ok, scores, neg_big)
    row_max = jnp.max(scores, axis=-1, keepdims=True)
    probs = jnp.exp(scores - row_max)
    return (probs.astype(jnp.bfloat16), jnp.sum(probs, axis=-1))


def pick_entries(table, picks):
    flat = table.reshape(-1)
    lane = math.gcd(flat.shape[0], 128)
    blocks = flat.reshape(flat.shape[0] // lane, lane)
    chosen = jnp.take(blocks, picks // lane, axis=0)
    lane_ids = jnp.arange(lane, dtype=jnp.int32)
    hit = lane_ids[None, :] == (picks % lane)[:, None]
    return jnp.sum(jnp.where(hit, chosen, jnp.float32(0.0)), axis=1)

def block_entries(blocks, block_of, lane_of):
    chosen = jnp.take(blocks, block_of, axis=0)
    lane_ids = jnp.arange(blocks.shape[1], dtype=jnp.int32)
    hit = lane_ids[None, :] == lane_of[:, None]
    return jnp.sum(jnp.where(hit, chosen, jnp.float32(0.0)), axis=1)


def group_picks(context_flat, grad_flat, picks, axis, levels):
    count = lax.axis_size(axis)
    levels = min(levels, count.bit_length() - 1)
    group = 1 << levels
    pair = jnp.stack([context_flat, grad_flat])
    for level in range(levels):
        step = 1 << level
        other = lax.ppermute(pair, axis, [(i, i ^ step) for i in range(count)])
        pair = jnp.concatenate([pair, other], axis=1)
    depth, table_rows = pair.shape[1], pair.shape[2]
    lane = math.gcd(table_rows, 128)
    grad_blocks = pair[1].reshape(depth, table_rows // lane, lane)
    table = jnp.einsum("ncl,nr->crl", grad_blocks, pair[0], preferred_element_type=jnp.float32)
    total = picks.shape[0]
    rows = -(-total // group)
    padded_picks = jnp.pad(picks, (0, rows * group - total))
    first = (lax.axis_index(axis) % group) * rows
    mine = lax.dynamic_slice(padded_picks, (first,), (rows,))
    block_of = (mine % table_rows) // lane * table_rows + mine // table_rows
    values = block_entries(table.reshape(-1, lane), block_of, mine % lane)
    spread = lax.dynamic_update_slice(jnp.zeros((rows * group,), jnp.float32), values, (first,))
    return spread[:total]


def butterfly_sum(value, axes):
    for axis in axes:
        count = lax.axis_size(axis)
        step = 1
        while step < count:
            pairs = [(i, i ^ step) for i in range(count)]
            value = value + lax.ppermute(value, axis, pairs)
            step *= 2
    return value


def attend(query, key, value, key_ok, score_scale):
    scores = jnp.dot(query, key.T, preferred_element_type=jnp.float32) * score_scale
    weights, denom = softmax_rows(scores, key_ok[None, :])
    out_rows = jnp.dot(weights, value, preferred_element_type=jnp.float32)
    return (out_rows / denom[:, None]).astype(jnp.bfloat16)


def head_attention(queries, key_rows, value_rows, utt_lengths, seq_index, score_scale, later):
    local_utts, frames_dev, width = queries.shape
    head_size = width // HEADS
    seq_count = HEADS * local_utts
    full_frames = frames_dev * seq_count
    stacked = jnp.stack([queries, key_rows, value_rows])
    stacked = stacked.reshape(3, local_utts, frames_dev, HEADS, head_size)
    stacked = stacked.transpose(3, 1, 0, 2, 4).reshape(seq_count, 3, frames_dev, head_size)
    gathered = lax.all_to_all(stacked, "seq", 0, 0, tiled=True)
    gathered, later = lax.optimization_barrier((gathered, later))
    gathered = gathered.transpose(1, 0, 2, 3).reshape(3, full_frames, head_size)
    length = utt_lengths[seq_index % local_utts]
    key_ok = jnp.arange(full_frames, dtype=jnp.int32) < length
    out_rows = attend(gathered[0], gathered[1], gathered[2], key_ok, score_scale)
    out_rows = out_rows.reshape(seq_count, frames_dev, head_size)
    back = lax.all_to_all(out_rows, "seq", 0, 0, tiled=True)
    back = back.reshape(HEADS, local_utts, frames_dev, head_size).transpose(1, 2, 0, 3)
    return back.reshape(local_utts, frames_dev, width), later


def frame_attention(queries, key_rows, value_rows, utt_lengths, score_scale):
    local_utts, frames_dev, width = queries.shape
    head_size = width // HEADS
    all_keys = lax.all_gather(key_rows, "seq", axis=1, tiled=True)
    all_values = lax.all_gather(value_rows, "seq", axis=1, tiled=True)
    full_frames = all_keys.shape[1]
    full_ids = jnp.arange(full_frames, dtype=jnp.int32)

    def one_utt(item):
        query_utt, key_utt, value_utt, length_utt = item
        query_heads = query_utt.reshape(frames_dev, HEADS, head_size)
        key_heads = key_utt.reshape(full_frames, HEADS, head_size)
        value_heads = value_utt.reshape(full_frames, HEADS, head_size)
        scores = (
            jnp.einsum("qhd,khd->hqk", query_heads, key_heads, preferred_element_type=jnp.float32)
            * score_scale
        )
        weights, denom = softmax_rows(scores, (full_ids < length_utt)[None, None, :])
        out_rows = jnp.einsum(
            "hqk,khd->qhd", weights, value_heads, preferred_element_type=jnp.float32
        )
        out_rows = out_rows / denom.transpose(1, 0)[:, :, None]
        return out_rows.astype(jnp.bfloat16).reshape(frames_dev, width)

    return lax.map(one_utt, (queries, all_keys, all_values, utt_lengths))


def on_device(
    queries,
    key_rows,
    value_rows,
    layer_input,
    utt_lengths,
    out_weight,
    conv_kernel,
    conv_cotangent,
    pick_weight,
    pick_kernel,
):
    local_utts, frames_dev, width = queries.shape
    seq_count = lax.axis_size("seq")
    full_frames = frames_dev * seq_count
    head_size = width // HEADS
    score_scale = 1.0 / math.sqrt(head_size)
    first_frame = lax.axis_index("seq") * frames_dev
    local_ids = first_frame + jnp.arange(frames_dev, dtype=jnp.int32)
    valid_rows = (local_ids[None, :] < utt_lengths[:, None]).astype(jnp.float32)
    seq_index = lax.axis_index("seq")
    if HEADS * local_utts == seq_count:
        context, conv_cotangent = head_attention(
            queries, key_rows, value_rows, utt_lengths, seq_index, score_scale, conv_cotangent
        )
    else:
        context = frame_attention(queries, key_rows, value_rows, utt_lengths, score_scale)
    context_flat = context.reshape(local_utts * frames_dev, width)
    projected = jnp.dot(context_flat, out_weight, preferred_element_type=jnp.float32).reshape(
        local_utts, frames_dev, width
    )
    hidden = ((layer_input.astype(jnp.float32) + projected) * valid_rows[:, :, None]).astype(
        jnp.bfloat16
    )
    tap_count = conv_kernel.shape[0]
    half_taps = (tap_count - 1) // 2
    kernel_f = conv_kernel.astype(jnp.float32)
    hidden_pad = padded(hidden, (("seq", 1),), half_taps)
    cot_f = conv_cotangent.astype(jnp.float32)
    conv_sum = jnp.zeros((local_utts, frames_dev, width), jnp.float32)
    kernel_rows = []
    for offset in range(tap_count):
        window = hidden_pad[:, offset : offset + frames_dev].astype(jnp.float32)
        conv_sum = conv_sum + kernel_f[offset] * window
        kernel_rows.append(jnp.sum(window * cot_f, axis=(0, 1)))
    conv_out = conv_sum.astype(jnp.bfloat16)
    kernel_grad = jnp.stack(kernel_rows)
    cot_pad = padded(conv_cotangent, (("seq", 1),), half_taps).astype(jnp.float32)
    back_sum = jnp.zeros((local_utts, frames_dev, width), jnp.float32)
    for offset in range(tap_count):
        begin = 2 * half_taps - offset
        back_sum = back_sum + kernel_f[offset] * cot_pad[:, begin : begin + frames_dev]
    hidden_grad = (back_sum * valid_rows[:, :, None]).astype(jnp.bfloat16)
    grad_flat = hidden_grad.reshape(local_utts * frames_dev, width)
    context_grad = lax.dot_general(
        grad_flat, out_weight, (((1,), (1,)), ((), ())), preferred_element_type=jnp.float32
    )
    context_grad = context_grad.reshape(local_utts, frames_dev, width).astype(jnp.bfloat16)
    weight_vals = group_picks(context_flat, grad_flat, pick_weight, "dp", 1)
    kernel_vals = pick_entries(kernel_grad, pick_kernel)
    joined = butterfly_sum(jnp.concatenate([weight_vals, kernel_vals]), ("dp", "seq"))
    weight_sum, kernel_sum = joined[: weight_vals.shape[0]], joined[weight_vals.shape[0] :]
    total_slots = local_utts * lax.axis_size("dp") * full_frames
    norm_factor = 1.0 / math.sqrt(total_slots)
    return (conv_out, context_grad, weight_sum * norm_factor, kernel_sum * norm_factor)


def solution(mesh):
    placed = (
        P("dp", "seq", None),
        P("dp", "seq", None),
        P("dp", "seq", None),
        P("dp", "seq", None),
        P("dp"),
        P(),
        P(),
        P("dp", "seq", None),
        P(),
        P(),
    )
    return jax.shard_map(
        on_device,
        mesh=mesh,
        in_specs=placed,
        out_specs=(P("dp", "seq", None), P("dp", "seq", None), P(), P()),
        check_vma=False,
    )
```

```python
import math

import jax
import jax.numpy as jnp
from jax import lax
from jax.sharding import PartitionSpec as P

HEADS = 16


neg_big = -1e30


def padded(value, sides, width):
    for axis, dim in sides:
        count, length = (lax.axis_size(axis), value.shape[dim])
        up = [(i, (i + 1) % count) for i in range(count - 1)]
        down = [(j, i) for i, j in up]
        last = lax.slice_in_dim(value, length - width, length, axis=dim)
        leading = lax.slice_in_dim(value, 0, width, axis=dim)
        before = lax.ppermute(last, axis, up)
        after = lax.ppermute(leading, axis, down)
        value = jnp.concatenate([before, value, after], axis=dim)
    return value


def softmax_rows(scores, key_ok):
    scores = jnp.where(key_ok, scores, neg_big)
    row_max = jnp.max(scores, axis=-1, keepdims=True)
    probs = jnp.exp(scores - row_max)
    return (probs.astype(jnp.bfloat16), jnp.sum(probs, axis=-1))


def pick_entries(table, picks):
    flat = table.reshape(-1)
    lane = math.gcd(flat.shape[0], 128)
    blocks = flat.reshape(flat.shape[0] // lane, lane)
    chosen = jnp.take(blocks, picks // lane, axis=0)
    lane_ids = jnp.arange(lane, dtype=jnp.int32)
    hit = lane_ids[None, :] == (picks % lane)[:, None]
    return jnp.sum(jnp.where(hit, chosen, jnp.float32(0.0)), axis=1)

def block_entries(blocks, block_of, lane_of):
    chosen = jnp.take(blocks, block_of, axis=0)
    lane_ids = jnp.arange(blocks.shape[1], dtype=jnp.int32)
    hit = lane_ids[None, :] == lane_of[:, None]
    return jnp.sum(jnp.where(hit, chosen, jnp.float32(0.0)), axis=1)


def group_picks(context_flat, grad_flat, picks, axis, levels):
    count = lax.axis_size(axis)
    levels = min(levels, count.bit_length() - 1)
    group = 1 << levels
    pair = jnp.stack([context_flat, grad_flat])
    for level in range(levels):
        step = 1 << level
        other = lax.ppermute(pair, axis, [(i, i ^ step) for i in range(count)])
        pair = jnp.concatenate([pair, other], axis=1)
    depth, table_rows = pair.shape[1], pair.shape[2]
    lane = math.gcd(table_rows, 128)
    grad_blocks = pair[1].reshape(depth, table_rows // lane, lane)
    table = jnp.einsum("ncl,nr->crl", grad_blocks, pair[0], preferred_element_type=jnp.float32)
    total = picks.shape[0]
    rows = -(-total // group)
    padded_picks = jnp.pad(picks, (0, rows * group - total))
    first = (lax.axis_index(axis) % group) * rows
    mine = lax.dynamic_slice(padded_picks, (first,), (rows,))
    block_of = (mine % table_rows) // lane * table_rows + mine // table_rows
    values = block_entries(table.reshape(-1, lane), block_of, mine % lane)
    spread = lax.dynamic_update_slice(jnp.zeros((rows * group,), jnp.float32), values, (first,))
    return spread[:total]


def butterfly_sum(value, axes):
    for axis in axes:
        count = lax.axis_size(axis)
        step = 1
        while step < count:
            pairs = [(i, i ^ step) for i in range(count)]
            value = value + lax.ppermute(value, axis, pairs)
            step *= 2
    return value


def attend(query, key, value, key_ok, score_scale):
    scores = jnp.dot(query, key.T, preferred_element_type=jnp.float32) * score_scale
    weights, denom = softmax_rows(scores, key_ok[None, :])
    out_rows = jnp.dot(weights, value, preferred_element_type=jnp.float32)
    return (out_rows / denom[:, None]).astype(jnp.bfloat16)


def lane_dense_all_to_all(value):
    chunk = math.prod(value.shape[1:])
    if chunk % 128:
        return lax.all_to_all(value, "seq", 0, 0, tiled=True)
    dense = value.reshape(value.shape[0], chunk // 128, 128)
    return lax.all_to_all(dense, "seq", 0, 0, tiled=True).reshape(value.shape)


def head_attention(queries, key_rows, value_rows, utt_lengths, seq_index, score_scale, later):
    local_utts, frames_dev, width = queries.shape
    head_size = width // HEADS
    seq_count = HEADS * local_utts
    full_frames = frames_dev * seq_count
    stacked = jnp.stack([queries, key_rows, value_rows])
    stacked = stacked.reshape(3, local_utts, frames_dev, HEADS, head_size)
    stacked = stacked.transpose(3, 1, 0, 2, 4).reshape(seq_count, 3, frames_dev, head_size)
    gathered = lane_dense_all_to_all(stacked)
    gathered, later = lax.optimization_barrier((gathered, later))
    gathered = gathered.transpose(1, 0, 2, 3).reshape(3, full_frames, head_size)
    length = utt_lengths[seq_index % local_utts]
    key_ok = jnp.arange(full_frames, dtype=jnp.int32) < length
    out_rows = attend(gathered[0], gathered[1], gathered[2], key_ok, score_scale)
    out_rows = out_rows.reshape(seq_count, frames_dev, head_size)
    back = lane_dense_all_to_all(out_rows)
    back = back.reshape(HEADS, local_utts, frames_dev, head_size).transpose(1, 2, 0, 3)
    return back.reshape(local_utts, frames_dev, width), later


def frame_attention(queries, key_rows, value_rows, utt_lengths, score_scale):
    local_utts, frames_dev, width = queries.shape
    head_size = width // HEADS
    all_keys = lax.all_gather(key_rows, "seq", axis=1, tiled=True)
    all_values = lax.all_gather(value_rows, "seq", axis=1, tiled=True)
    full_frames = all_keys.shape[1]
    full_ids = jnp.arange(full_frames, dtype=jnp.int32)

    def one_utt(item):
        query_utt, key_utt, value_utt, length_utt = item
        query_heads = query_utt.reshape(frames_dev, HEADS, head_size)
        key_heads = key_utt.reshape(full_frames, HEADS, head_size)
        value_heads = value_utt.reshape(full_frames, HEADS, head_size)
        scores = (
            jnp.einsum("qhd,khd->hqk", query_heads, key_heads, preferred_element_type=jnp.float32)
            * score_scale
        )
        weights, denom = softmax_rows(scores, (full_ids < length_utt)[None, None, :])
        out_rows = jnp.einsum(
            "hqk,khd->qhd", weights, value_heads, preferred_element_type=jnp.float32
        )
        out_rows = out_rows / denom.transpose(1, 0)[:, :, None]
        return out_rows.astype(jnp.bfloat16).reshape(frames_dev, width)

    return lax.map(one_utt, (queries, all_keys, all_values, utt_lengths))


def on_device(
    queries,
    key_rows,
    value_rows,
    layer_input,
    utt_lengths,
    out_weight,
    conv_kernel,
    conv_cotangent,
    pick_weight,
    pick_kernel,
):
    local_utts, frames_dev, width = queries.shape
    seq_count = lax.axis_size("seq")
    full_frames = frames_dev * seq_count
    head_size = width // HEADS
    score_scale = 1.0 / math.sqrt(head_size)
    first_frame = lax.axis_index("seq") * frames_dev
    local_ids = first_frame + jnp.arange(frames_dev, dtype=jnp.int32)
    valid_rows = (local_ids[None, :] < utt_lengths[:, None]).astype(jnp.float32)
    seq_index = lax.axis_index("seq")
    if HEADS * local_utts == seq_count:
        context, conv_cotangent = head_attention(
            queries, key_rows, value_rows, utt_lengths, seq_index, score_scale, conv_cotangent
        )
    else:
        context = frame_attention(queries, key_rows, value_rows, utt_lengths, score_scale)
    context_flat = context.reshape(local_utts * frames_dev, width)
    projected = jnp.dot(context_flat, out_weight, preferred_element_type=jnp.float32).reshape(
        local_utts, frames_dev, width
    )
    hidden = ((layer_input.astype(jnp.float32) + projected) * valid_rows[:, :, None]).astype(
        jnp.bfloat16
    )
    tap_count = conv_kernel.shape[0]
    half_taps = (tap_count - 1) // 2
    kernel_f = conv_kernel.astype(jnp.float32)
    hidden_pad = padded(hidden, (("seq", 1),), half_taps)
    cot_f = conv_cotangent.astype(jnp.float32)
    conv_sum = jnp.zeros((local_utts, frames_dev, width), jnp.float32)
    kernel_rows = []
    for offset in range(tap_count):
        window = hidden_pad[:, offset : offset + frames_dev].astype(jnp.float32)
        conv_sum = conv_sum + kernel_f[offset] * window
        kernel_rows.append(jnp.sum(window * cot_f, axis=(0, 1)))
    conv_out = conv_sum.astype(jnp.bfloat16)
    kernel_grad = jnp.stack(kernel_rows)
    cot_pad = padded(conv_cotangent, (("seq", 1),), half_taps).astype(jnp.float32)
    back_sum = jnp.zeros((local_utts, frames_dev, width), jnp.float32)
    for offset in range(tap_count):
        begin = 2 * half_taps - offset
        back_sum = back_sum + kernel_f[offset] * cot_pad[:, begin : begin + frames_dev]
    hidden_grad = (back_sum * valid_rows[:, :, None]).astype(jnp.bfloat16)
    grad_flat = hidden_grad.reshape(local_utts * frames_dev, width)
    context_grad = lax.dot_general(
        grad_flat, out_weight, (((1,), (1,)), ((), ())), preferred_element_type=jnp.float32
    )
    context_grad = context_grad.reshape(local_utts, frames_dev, width).astype(jnp.bfloat16)
    weight_vals = group_picks(context_flat, grad_flat, pick_weight, "dp", 1)
    kernel_vals = pick_entries(kernel_grad, pick_kernel)
    joined = butterfly_sum(jnp.concatenate([weight_vals, kernel_vals]), ("dp", "seq"))
    weight_sum, kernel_sum = joined[: weight_vals.shape[0]], joined[weight_vals.shape[0] :]
    total_slots = local_utts * lax.axis_size("dp") * full_frames
    norm_factor = 1.0 / math.sqrt(total_slots)
    return (conv_out, context_grad, weight_sum * norm_factor, kernel_sum * norm_factor)


def solution(mesh):
    placed = (
        P("dp", "seq", None),
        P("dp", "seq", None),
        P("dp", "seq", None),
        P("dp", "seq", None),
        P("dp"),
        P(),
        P(),
        P("dp", "seq", None),
        P(),
        P(),
    )
    return jax.shard_map(
        on_device,
        mesh=mesh,
        in_specs=placed,
        out_specs=(P("dp", "seq", None), P("dp", "seq", None), P(), P()),
        check_vma=False,
    )
```

```python
import math

import jax
import jax.numpy as jnp
from jax import lax
from jax.sharding import PartitionSpec as P

HEADS = 16


neg_big = -1e30


def padded(value, sides, width):
    for axis, dim in sides:
        count, length = (lax.axis_size(axis), value.shape[dim])
        up = [(i, (i + 1) % count) for i in range(count - 1)]
        down = [(j, i) for i, j in up]
        last = lax.slice_in_dim(value, length - width, length, axis=dim)
        leading = lax.slice_in_dim(value, 0, width, axis=dim)
        before = lax.ppermute(last, axis, up)
        after = lax.ppermute(leading, axis, down)
        value = jnp.concatenate([before, value, after], axis=dim)
    return value


def softmax_rows(scores, key_ok):
    scores = jnp.where(key_ok, scores, neg_big)
    row_max = jnp.max(scores, axis=-1, keepdims=True)
    probs = jnp.exp(scores - row_max)
    return (probs.astype(jnp.bfloat16), jnp.sum(probs, axis=-1))


def pick_entries(table, picks):
    flat = table.reshape(-1)
    lane = math.gcd(flat.shape[0], 128)
    blocks = flat.reshape(flat.shape[0] // lane, lane)
    chosen = jnp.take(blocks, picks // lane, axis=0)
    lane_ids = jnp.arange(lane, dtype=jnp.int32)
    hit = lane_ids[None, :] == (picks % lane)[:, None]
    return jnp.sum(jnp.where(hit, chosen, jnp.float32(0.0)), axis=1)

def block_entries(blocks, block_of, lane_of):
    chosen = jnp.take(blocks, block_of, axis=0)
    lane_ids = jnp.arange(blocks.shape[1], dtype=jnp.int32)
    hit = lane_ids[None, :] == lane_of[:, None]
    return jnp.sum(jnp.where(hit, chosen, jnp.float32(0.0)), axis=1)


def group_picks(context_flat, grad_flat, picks, axis, levels):
    count = lax.axis_size(axis)
    levels = min(levels, count.bit_length() - 1)
    group = 1 << levels
    pair = jnp.stack([context_flat, grad_flat])
    for level in range(levels):
        step = 1 << level
        other = lax.ppermute(pair, axis, [(i, i ^ step) for i in range(count)])
        pair = jnp.concatenate([pair, other], axis=1)
    depth, table_rows = pair.shape[1], pair.shape[2]
    lane = math.gcd(table_rows, 128)
    grad_blocks = pair[1].reshape(depth, table_rows // lane, lane)
    table = jnp.einsum("ncl,nr->crl", grad_blocks, pair[0], preferred_element_type=jnp.float32)
    total = picks.shape[0]
    rows = -(-total // group)
    padded_picks = jnp.pad(picks, (0, rows * group - total))
    first = (lax.axis_index(axis) % group) * rows
    mine = lax.dynamic_slice(padded_picks, (first,), (rows,))
    block_of = (mine % table_rows) // lane * table_rows + mine // table_rows
    values = block_entries(table.reshape(-1, lane), block_of, mine % lane)
    return values, lax.axis_index(axis) % group


def butterfly_sum(value, axes, first_step=None):
    first_step = first_step or {}
    for axis in axes:
        count = lax.axis_size(axis)
        step = first_step.get(axis, 1)
        while step < count:
            pairs = [(i, i ^ step) for i in range(count)]
            value = value + lax.ppermute(value, axis, pairs)
            step *= 2
    return value


def attend(query, key, value, key_ok, score_scale):
    scores = jnp.dot(query, key.T, preferred_element_type=jnp.float32) * score_scale
    weights, denom = softmax_rows(scores, key_ok[None, :])
    out_rows = jnp.dot(weights, value, preferred_element_type=jnp.float32)
    return (out_rows / denom[:, None]).astype(jnp.bfloat16)


def lane_dense_all_to_all(value):
    chunk = math.prod(value.shape[1:])
    if chunk % 128:
        return lax.all_to_all(value, "seq", 0, 0, tiled=True)
    dense = value.reshape(value.shape[0], chunk // 128, 128)
    return lax.all_to_all(dense, "seq", 0, 0, tiled=True).reshape(value.shape)


def head_attention(queries, key_rows, value_rows, utt_lengths, seq_index, score_scale, later):
    local_utts, frames_dev, width = queries.shape
    head_size = width // HEADS
    seq_count = HEADS * local_utts
    full_frames = frames_dev * seq_count
    stacked = jnp.stack([queries, key_rows, value_rows])
    stacked = stacked.reshape(3, local_utts, frames_dev, HEADS, head_size)
    stacked = stacked.transpose(3, 1, 0, 2, 4).reshape(seq_count, 3, frames_dev, head_size)
    gathered = lane_dense_all_to_all(stacked)
    gathered, later = lax.optimization_barrier((gathered, later))
    gathered = gathered.transpose(1, 0, 2, 3).reshape(3, full_frames, head_size)
    length = utt_lengths[seq_index % local_utts]
    key_ok = jnp.arange(full_frames, dtype=jnp.int32) < length
    out_rows = attend(gathered[0], gathered[1], gathered[2], key_ok, score_scale)
    out_rows = out_rows.reshape(seq_count, frames_dev, head_size)
    back = lane_dense_all_to_all(out_rows)
    back = back.reshape(HEADS, local_utts, frames_dev, head_size).transpose(1, 2, 0, 3)
    return back.reshape(local_utts, frames_dev, width), later


def frame_attention(queries, key_rows, value_rows, utt_lengths, score_scale):
    local_utts, frames_dev, width = queries.shape
    head_size = width // HEADS
    all_keys = lax.all_gather(key_rows, "seq", axis=1, tiled=True)
    all_values = lax.all_gather(value_rows, "seq", axis=1, tiled=True)
    full_frames = all_keys.shape[1]
    full_ids = jnp.arange(full_frames, dtype=jnp.int32)

    def one_utt(item):
        query_utt, key_utt, value_utt, length_utt = item
        query_heads = query_utt.reshape(frames_dev, HEADS, head_size)
        key_heads = key_utt.reshape(full_frames, HEADS, head_size)
        value_heads = value_utt.reshape(full_frames, HEADS, head_size)
        scores = (
            jnp.einsum("qhd,khd->hqk", query_heads, key_heads, preferred_element_type=jnp.float32)
            * score_scale
        )
        weights, denom = softmax_rows(scores, (full_ids < length_utt)[None, None, :])
        out_rows = jnp.einsum(
            "hqk,khd->qhd", weights, value_heads, preferred_element_type=jnp.float32
        )
        out_rows = out_rows / denom.transpose(1, 0)[:, :, None]
        return out_rows.astype(jnp.bfloat16).reshape(frames_dev, width)

    return lax.map(one_utt, (queries, all_keys, all_values, utt_lengths))


def on_device(
    queries,
    key_rows,
    value_rows,
    layer_input,
    utt_lengths,
    out_weight,
    conv_kernel,
    conv_cotangent,
    pick_weight,
    pick_kernel,
):
    local_utts, frames_dev, width = queries.shape
    seq_count = lax.axis_size("seq")
    full_frames = frames_dev * seq_count
    head_size = width // HEADS
    score_scale = 1.0 / math.sqrt(head_size)
    first_frame = lax.axis_index("seq") * frames_dev
    local_ids = first_frame + jnp.arange(frames_dev, dtype=jnp.int32)
    valid_rows = (local_ids[None, :] < utt_lengths[:, None]).astype(jnp.float32)
    seq_index = lax.axis_index("seq")
    if HEADS * local_utts == seq_count:
        context, conv_cotangent = head_attention(
            queries, key_rows, value_rows, utt_lengths, seq_index, score_scale, conv_cotangent
        )
    else:
        context = frame_attention(queries, key_rows, value_rows, utt_lengths, score_scale)
    context_flat = context.reshape(local_utts * frames_dev, width)
    projected = jnp.dot(context_flat, out_weight, preferred_element_type=jnp.float32).reshape(
        local_utts, frames_dev, width
    )
    hidden = ((layer_input.astype(jnp.float32) + projected) * valid_rows[:, :, None]).astype(
        jnp.bfloat16
    )
    tap_count = conv_kernel.shape[0]
    half_taps = (tap_count - 1) // 2
    kernel_f = conv_kernel.astype(jnp.float32)
    hidden_pad = padded(hidden, (("seq", 1),), half_taps)
    cot_f = conv_cotangent.astype(jnp.float32)
    conv_sum = jnp.zeros((local_utts, frames_dev, width), jnp.float32)
    kernel_rows = []
    for offset in range(tap_count):
        window = hidden_pad[:, offset : offset + frames_dev].astype(jnp.float32)
        conv_sum = conv_sum + kernel_f[offset] * window
        kernel_rows.append(jnp.sum(window * cot_f, axis=(0, 1)))
    conv_out = conv_sum.astype(jnp.bfloat16)
    kernel_grad = jnp.stack(kernel_rows)
    cot_pad = padded(conv_cotangent, (("seq", 1),), half_taps).astype(jnp.float32)
    back_sum = jnp.zeros((local_utts, frames_dev, width), jnp.float32)
    for offset in range(tap_count):
        begin = 2 * half_taps - offset
        back_sum = back_sum + kernel_f[offset] * cot_pad[:, begin : begin + frames_dev]
    hidden_grad = (back_sum * valid_rows[:, :, None]).astype(jnp.bfloat16)
    grad_flat = hidden_grad.reshape(local_utts * frames_dev, width)
    context_grad = lax.dot_general(
        grad_flat, out_weight, (((1,), (1,)), ((), ())), preferred_element_type=jnp.float32
    )
    context_grad = context_grad.reshape(local_utts, frames_dev, width).astype(jnp.bfloat16)
    weight_half, member = group_picks(context_flat, grad_flat, pick_weight, "dp", 1)
    kernel_vals = pick_entries(kernel_grad, pick_kernel)
    half_count = weight_half.shape[0]
    joined = butterfly_sum(jnp.concatenate([weight_half, kernel_vals]), ("dp", "seq"), {"dp": 2})
    dp_count = lax.axis_size("dp")
    other = lax.ppermute(joined, "dp", [(i, i ^ 1) for i in range(dp_count)])
    low, high = jnp.where(member == 0, joined, other), jnp.where(member == 0, other, joined)
    total = pick_weight.shape[0]
    weight_sum = jnp.concatenate([low[:half_count], high[:half_count]])[:total]
    kernel_sum = low[half_count:] + high[half_count:]
    total_slots = local_utts * lax.axis_size("dp") * full_frames
    norm_factor = 1.0 / math.sqrt(total_slots)
    return (conv_out, context_grad, weight_sum * norm_factor, kernel_sum * norm_factor)


def solution(mesh):
    placed = (
        P("dp", "seq", None),
        P("dp", "seq", None),
        P("dp", "seq", None),
        P("dp", "seq", None),
        P("dp"),
        P(),
        P(),
        P("dp", "seq", None),
        P(),
        P(),
    )
    return jax.shard_map(
        on_device,
        mesh=mesh,
        in_specs=placed,
        out_specs=(P("dp", "seq", None), P("dp", "seq", None), P(), P()),
        check_vma=False,
    )
```

```python
import math

import jax
import jax.numpy as jnp
from jax import lax
from jax.sharding import PartitionSpec as P

HEADS = 16


neg_big = -1e30


def padded(value, sides, width):
    for axis, dim in sides:
        count, length = (lax.axis_size(axis), value.shape[dim])
        up = [(i, (i + 1) % count) for i in range(count - 1)]
        down = [(j, i) for i, j in up]
        last = lax.slice_in_dim(value, length - width, length, axis=dim)
        leading = lax.slice_in_dim(value, 0, width, axis=dim)
        before = lax.ppermute(last, axis, up)
        after = lax.ppermute(leading, axis, down)
        value = jnp.concatenate([before, value, after], axis=dim)
    return value


def softmax_rows(scores, key_ok):
    scores = jnp.where(key_ok, scores, neg_big)
    row_max = jnp.max(scores, axis=-1, keepdims=True)
    probs = jnp.exp(scores - row_max)
    return (probs.astype(jnp.bfloat16), jnp.sum(probs, axis=-1))


def pick_entries(table, picks):
    flat = table.reshape(-1)
    lane = math.gcd(flat.shape[0], 128)
    blocks = flat.reshape(flat.shape[0] // lane, lane)
    chosen = jnp.take(blocks, picks // lane, axis=0)
    lane_ids = jnp.arange(lane, dtype=jnp.int32)
    hit = lane_ids[None, :] == (picks % lane)[:, None]
    return jnp.sum(jnp.where(hit, chosen, jnp.float32(0.0)), axis=1)

def block_entries(blocks, block_of, lane_of):
    chosen = jnp.take(blocks, block_of, axis=0)
    lane_ids = jnp.arange(blocks.shape[1], dtype=jnp.int32)
    hit = lane_ids[None, :] == lane_of[:, None]
    return jnp.sum(jnp.where(hit, chosen, jnp.float32(0.0)), axis=1)


def group_picks(context_flat, grad_flat, picks, axis, levels):
    count = lax.axis_size(axis)
    levels = min(levels, count.bit_length() - 1)
    group = 1 << levels
    pair = jnp.stack([context_flat, grad_flat])
    for level in range(levels):
        step = 1 << level
        other = lax.ppermute(pair, axis, [(i, i ^ step) for i in range(count)])
        pair = jnp.concatenate([pair, other], axis=1)
    depth, table_rows = pair.shape[1], pair.shape[2]
    lane = math.gcd(table_rows, 128)
    grad_blocks = pair[1].reshape(depth, table_rows // lane, lane)
    table = jnp.einsum("ncl,nr->crl", grad_blocks, pair[0], preferred_element_type=jnp.float32)
    total = picks.shape[0]
    rows = -(-total // group)
    padded_picks = jnp.pad(picks, (0, rows * group - total))
    first = (lax.axis_index(axis) % group) * rows
    mine = lax.dynamic_slice(padded_picks, (first,), (rows,))
    block_of = (mine % table_rows) // lane * table_rows + mine // table_rows
    values = block_entries(table.reshape(-1, lane), block_of, mine % lane)
    return values, lax.axis_index(axis) % group


def butterfly_sum(value, axes, first_step=None):
    first_step = first_step or {}
    for axis in axes:
        count = lax.axis_size(axis)
        step = first_step.get(axis, 1)
        while step < count:
            pairs = [(i, i ^ step) for i in range(count)]
            value = value + lax.ppermute(value, axis, pairs)
            step *= 2
    return value


def attend(query, key, value, key_ok, score_scale):
    scores = jnp.dot(query, key.T, preferred_element_type=jnp.float32) * score_scale
    weights, denom = softmax_rows(scores, key_ok[None, :])
    out_rows = jnp.dot(weights, value, preferred_element_type=jnp.float32)
    return (out_rows / denom[:, None]).astype(jnp.bfloat16)


def lane_dense_all_to_all(value):
    chunk = math.prod(value.shape[1:])
    if chunk % 128:
        return lax.all_to_all(value, "seq", 0, 0, tiled=True)
    dense = value.reshape(value.shape[0], chunk // 128, 128)
    return lax.all_to_all(dense, "seq", 0, 0, tiled=True).reshape(value.shape)


def head_attention(queries, key_rows, value_rows, utt_lengths, seq_index, score_scale, later):
    local_utts, frames_dev, width = queries.shape
    head_size = width // HEADS
    seq_count = HEADS * local_utts
    full_frames = frames_dev * seq_count
    stacked = jnp.stack([queries, key_rows, value_rows])
    stacked = stacked.reshape(3, local_utts, frames_dev, HEADS, head_size)
    stacked = stacked.transpose(3, 1, 0, 2, 4).reshape(seq_count, 3, frames_dev, head_size)
    gathered = lane_dense_all_to_all(stacked)
    gathered, later = lax.optimization_barrier((gathered, later))
    gathered = gathered.transpose(1, 0, 2, 3).reshape(3, full_frames, head_size)
    length = utt_lengths[seq_index % local_utts]
    key_ok = jnp.arange(full_frames, dtype=jnp.int32) < length
    out_rows = attend(gathered[0], gathered[1], gathered[2], key_ok, score_scale)
    out_rows = out_rows.reshape(seq_count, frames_dev, head_size)
    back = lane_dense_all_to_all(out_rows)
    back = back.reshape(HEADS, local_utts, frames_dev, head_size).transpose(1, 2, 0, 3)
    return back.reshape(local_utts, frames_dev, width), later


def frame_attention(queries, key_rows, value_rows, utt_lengths, score_scale):
    local_utts, frames_dev, width = queries.shape
    head_size = width // HEADS
    all_keys = lax.all_gather(key_rows, "seq", axis=1, tiled=True)
    all_values = lax.all_gather(value_rows, "seq", axis=1, tiled=True)
    full_frames = all_keys.shape[1]
    full_ids = jnp.arange(full_frames, dtype=jnp.int32)

    def one_utt(item):
        query_utt, key_utt, value_utt, length_utt = item
        query_heads = query_utt.reshape(frames_dev, HEADS, head_size)
        key_heads = key_utt.reshape(full_frames, HEADS, head_size)
        value_heads = value_utt.reshape(full_frames, HEADS, head_size)
        scores = (
            jnp.einsum("qhd,khd->hqk", query_heads, key_heads, preferred_element_type=jnp.float32)
            * score_scale
        )
        weights, denom = softmax_rows(scores, (full_ids < length_utt)[None, None, :])
        out_rows = jnp.einsum(
            "hqk,khd->qhd", weights, value_heads, preferred_element_type=jnp.float32
        )
        out_rows = out_rows / denom.transpose(1, 0)[:, :, None]
        return out_rows.astype(jnp.bfloat16).reshape(frames_dev, width)

    return lax.map(one_utt, (queries, all_keys, all_values, utt_lengths))


def on_device(
    queries,
    key_rows,
    value_rows,
    layer_input,
    utt_lengths,
    out_weight,
    conv_kernel,
    conv_cotangent,
    pick_weight,
    pick_kernel,
):
    local_utts, frames_dev, width = queries.shape
    seq_count = lax.axis_size("seq")
    full_frames = frames_dev * seq_count
    head_size = width // HEADS
    score_scale = 1.0 / math.sqrt(head_size)
    first_frame = lax.axis_index("seq") * frames_dev
    local_ids = first_frame + jnp.arange(frames_dev, dtype=jnp.int32)
    valid_rows = (local_ids[None, :] < utt_lengths[:, None]).astype(jnp.float32)
    seq_index = lax.axis_index("seq")
    if HEADS * local_utts == seq_count:
        context, conv_cotangent = head_attention(
            queries, key_rows, value_rows, utt_lengths, seq_index, score_scale, conv_cotangent
        )
    else:
        context = frame_attention(queries, key_rows, value_rows, utt_lengths, score_scale)
    context_flat = context.reshape(local_utts * frames_dev, width)
    projected = jnp.dot(context_flat, out_weight, preferred_element_type=jnp.float32).reshape(
        local_utts, frames_dev, width
    )
    hidden = ((layer_input.astype(jnp.float32) + projected) * valid_rows[:, :, None]).astype(
        jnp.bfloat16
    )
    tap_count = conv_kernel.shape[0]
    half_taps = (tap_count - 1) // 2
    kernel_f = conv_kernel.astype(jnp.float32)
    both_pad = padded(jnp.stack([hidden, conv_cotangent]), (("seq", 2),), half_taps)
    hidden_pad = both_pad[0]
    cot_f = conv_cotangent.astype(jnp.float32)
    conv_sum = jnp.zeros((local_utts, frames_dev, width), jnp.float32)
    kernel_rows = []
    for offset in range(tap_count):
        window = hidden_pad[:, offset : offset + frames_dev].astype(jnp.float32)
        conv_sum = conv_sum + kernel_f[offset] * window
        kernel_rows.append(jnp.sum(window * cot_f, axis=(0, 1)))
    conv_out = conv_sum.astype(jnp.bfloat16)
    kernel_grad = jnp.stack(kernel_rows)
    cot_pad = both_pad[1].astype(jnp.float32)
    back_sum = jnp.zeros((local_utts, frames_dev, width), jnp.float32)
    for offset in range(tap_count):
        begin = 2 * half_taps - offset
        back_sum = back_sum + kernel_f[offset] * cot_pad[:, begin : begin + frames_dev]
    hidden_grad = (back_sum * valid_rows[:, :, None]).astype(jnp.bfloat16)
    grad_flat = hidden_grad.reshape(local_utts * frames_dev, width)
    context_grad = lax.dot_general(
        grad_flat, out_weight, (((1,), (1,)), ((), ())), preferred_element_type=jnp.float32
    )
    context_grad = context_grad.reshape(local_utts, frames_dev, width).astype(jnp.bfloat16)
    weight_half, member = group_picks(context_flat, grad_flat, pick_weight, "dp", 1)
    kernel_vals = pick_entries(kernel_grad, pick_kernel)
    half_count = weight_half.shape[0]
    joined = butterfly_sum(jnp.concatenate([weight_half, kernel_vals]), ("dp", "seq"), {"dp": 2})
    dp_count = lax.axis_size("dp")
    other = lax.ppermute(joined, "dp", [(i, i ^ 1) for i in range(dp_count)])
    low, high = jnp.where(member == 0, joined, other), jnp.where(member == 0, other, joined)
    total = pick_weight.shape[0]
    weight_sum = jnp.concatenate([low[:half_count], high[:half_count]])[:total]
    kernel_sum = low[half_count:] + high[half_count:]
    total_slots = local_utts * lax.axis_size("dp") * full_frames
    norm_factor = 1.0 / math.sqrt(total_slots)
    return (conv_out, context_grad, weight_sum * norm_factor, kernel_sum * norm_factor)


def solution(mesh):
    placed = (
        P("dp", "seq", None),
        P("dp", "seq", None),
        P("dp", "seq", None),
        P("dp", "seq", None),
        P("dp"),
        P(),
        P(),
        P("dp", "seq", None),
        P(),
        P(),
    )
    return jax.shard_map(
        on_device,
        mesh=mesh,
        in_specs=placed,
        out_specs=(P("dp", "seq", None), P("dp", "seq", None), P(), P()),
        check_vma=False,
    )
```

```python
import math

import jax
import jax.numpy as jnp
from jax import lax
from jax.sharding import PartitionSpec as P

HEADS = 16


neg_big = -1e30


def padded(value, sides, width):
    for axis, dim in sides:
        count, length = (lax.axis_size(axis), value.shape[dim])
        up = [(i, (i + 1) % count) for i in range(count - 1)]
        down = [(j, i) for i, j in up]
        last = lax.slice_in_dim(value, length - width, length, axis=dim)
        leading = lax.slice_in_dim(value, 0, width, axis=dim)
        before = lax.ppermute(last, axis, up)
        after = lax.ppermute(leading, axis, down)
        value = jnp.concatenate([before, value, after], axis=dim)
    return value


def softmax_rows(scores, key_ok):
    scores = jnp.where(key_ok, scores, neg_big)
    row_max = jnp.max(scores, axis=-1, keepdims=True)
    probs = jnp.exp(scores - row_max)
    return (probs.astype(jnp.bfloat16), jnp.sum(probs, axis=-1))


def pick_entries(table, picks):
    flat = table.reshape(-1)
    lane = math.gcd(flat.shape[0], 128)
    blocks = flat.reshape(flat.shape[0] // lane, lane)
    chosen = jnp.take(blocks, picks // lane, axis=0)
    lane_ids = jnp.arange(lane, dtype=jnp.int32)
    hit = lane_ids[None, :] == (picks % lane)[:, None]
    return jnp.sum(jnp.where(hit, chosen, jnp.float32(0.0)), axis=1)

def block_entries(blocks, block_of, lane_of):
    chosen = jnp.take(blocks, block_of, axis=0)
    lane_ids = jnp.arange(blocks.shape[1], dtype=jnp.int32)
    hit = lane_ids[None, :] == lane_of[:, None]
    masked = jnp.where(hit, chosen, jnp.float32(0.0))
    ones = jnp.ones((blocks.shape[1], blocks.shape[1]), jnp.float32)
    return jnp.dot(masked, ones, precision=lax.Precision.HIGHEST)[:, 0]


def group_picks(context_flat, grad_flat, picks, axis, levels):
    count = lax.axis_size(axis)
    levels = min(levels, count.bit_length() - 1)
    group = 1 << levels
    pair = jnp.stack([context_flat, grad_flat])
    for level in range(levels):
        step = 1 << level
        other = lax.ppermute(pair, axis, [(i, i ^ step) for i in range(count)])
        pair = jnp.concatenate([pair, other], axis=1)
    depth, table_rows = pair.shape[1], pair.shape[2]
    lane = math.gcd(table_rows, 128)
    grad_blocks = pair[1].reshape(depth, table_rows // lane, lane)
    table = jnp.einsum("ncl,nr->crl", grad_blocks, pair[0], preferred_element_type=jnp.float32)
    total = picks.shape[0]
    rows = -(-total // group)
    padded_picks = jnp.pad(picks, (0, rows * group - total))
    first = (lax.axis_index(axis) % group) * rows
    mine = lax.dynamic_slice(padded_picks, (first,), (rows,))
    block_of = (mine % table_rows) // lane * table_rows + mine // table_rows
    values = block_entries(table.reshape(-1, lane), block_of, mine % lane)
    return values, lax.axis_index(axis) % group


def butterfly_sum(value, axes, first_step=None):
    first_step = first_step or {}
    for axis in axes:
        count = lax.axis_size(axis)
        step = first_step.get(axis, 1)
        while step < count:
            pairs = [(i, i ^ step) for i in range(count)]
            value = value + lax.ppermute(value, axis, pairs)
            step *= 2
    return value


def attend(query, key, value, key_ok, score_scale):
    scores = jnp.dot(query, key.T, preferred_element_type=jnp.float32) * score_scale
    weights, denom = softmax_rows(scores, key_ok[None, :])
    out_rows = jnp.dot(weights, value, preferred_element_type=jnp.float32)
    return (out_rows / denom[:, None]).astype(jnp.bfloat16)


def lane_dense_all_to_all(value):
    chunk = math.prod(value.shape[1:])
    if chunk % 128:
        return lax.all_to_all(value, "seq", 0, 0, tiled=True)
    dense = value.reshape(value.shape[0], chunk // 128, 128)
    return lax.all_to_all(dense, "seq", 0, 0, tiled=True).reshape(value.shape)


def head_attention(queries, key_rows, value_rows, utt_lengths, seq_index, score_scale, later):
    local_utts, frames_dev, width = queries.shape
    head_size = width // HEADS
    seq_count = HEADS * local_utts
    full_frames = frames_dev * seq_count
    stacked = jnp.stack([queries, key_rows, value_rows])
    stacked = stacked.reshape(3, local_utts, frames_dev, HEADS, head_size)
    stacked = stacked.transpose(3, 1, 0, 2, 4).reshape(seq_count, 3, frames_dev, head_size)
    gathered = lane_dense_all_to_all(stacked)
    gathered, later = lax.optimization_barrier((gathered, later))
    gathered = gathered.transpose(1, 0, 2, 3).reshape(3, full_frames, head_size)
    length = utt_lengths[seq_index % local_utts]
    key_ok = jnp.arange(full_frames, dtype=jnp.int32) < length
    out_rows = attend(gathered[0], gathered[1], gathered[2], key_ok, score_scale)
    out_rows = out_rows.reshape(seq_count, frames_dev, head_size)
    back = lane_dense_all_to_all(out_rows)
    back = back.reshape(HEADS, local_utts, frames_dev, head_size).transpose(1, 2, 0, 3)
    return back.reshape(local_utts, frames_dev, width), later


def frame_attention(queries, key_rows, value_rows, utt_lengths, score_scale):
    local_utts, frames_dev, width = queries.shape
    head_size = width // HEADS
    all_keys = lax.all_gather(key_rows, "seq", axis=1, tiled=True)
    all_values = lax.all_gather(value_rows, "seq", axis=1, tiled=True)
    full_frames = all_keys.shape[1]
    full_ids = jnp.arange(full_frames, dtype=jnp.int32)

    def one_utt(item):
        query_utt, key_utt, value_utt, length_utt = item
        query_heads = query_utt.reshape(frames_dev, HEADS, head_size)
        key_heads = key_utt.reshape(full_frames, HEADS, head_size)
        value_heads = value_utt.reshape(full_frames, HEADS, head_size)
        scores = (
            jnp.einsum("qhd,khd->hqk", query_heads, key_heads, preferred_element_type=jnp.float32)
            * score_scale
        )
        weights, denom = softmax_rows(scores, (full_ids < length_utt)[None, None, :])
        out_rows = jnp.einsum(
            "hqk,khd->qhd", weights, value_heads, preferred_element_type=jnp.float32
        )
        out_rows = out_rows / denom.transpose(1, 0)[:, :, None]
        return out_rows.astype(jnp.bfloat16).reshape(frames_dev, width)

    return lax.map(one_utt, (queries, all_keys, all_values, utt_lengths))


def on_device(
    queries,
    key_rows,
    value_rows,
    layer_input,
    utt_lengths,
    out_weight,
    conv_kernel,
    conv_cotangent,
    pick_weight,
    pick_kernel,
):
    local_utts, frames_dev, width = queries.shape
    seq_count = lax.axis_size("seq")
    full_frames = frames_dev * seq_count
    head_size = width // HEADS
    score_scale = 1.0 / math.sqrt(head_size)
    first_frame = lax.axis_index("seq") * frames_dev
    local_ids = first_frame + jnp.arange(frames_dev, dtype=jnp.int32)
    valid_rows = (local_ids[None, :] < utt_lengths[:, None]).astype(jnp.float32)
    seq_index = lax.axis_index("seq")
    if HEADS * local_utts == seq_count:
        context, conv_cotangent = head_attention(
            queries, key_rows, value_rows, utt_lengths, seq_index, score_scale, conv_cotangent
        )
    else:
        context = frame_attention(queries, key_rows, value_rows, utt_lengths, score_scale)
    context_flat = context.reshape(local_utts * frames_dev, width)
    projected = jnp.dot(context_flat, out_weight, preferred_element_type=jnp.float32).reshape(
        local_utts, frames_dev, width
    )
    hidden = ((layer_input.astype(jnp.float32) + projected) * valid_rows[:, :, None]).astype(
        jnp.bfloat16
    )
    tap_count = conv_kernel.shape[0]
    half_taps = (tap_count - 1) // 2
    kernel_f = conv_kernel.astype(jnp.float32)
    both_pad = padded(jnp.stack([hidden, conv_cotangent]), (("seq", 2),), half_taps)
    hidden_pad = both_pad[0]
    cot_f = conv_cotangent.astype(jnp.float32)
    conv_sum = jnp.zeros((local_utts, frames_dev, width), jnp.float32)
    kernel_rows = []
    for offset in range(tap_count):
        window = hidden_pad[:, offset : offset + frames_dev].astype(jnp.float32)
        conv_sum = conv_sum + kernel_f[offset] * window
        kernel_rows.append(jnp.sum(window * cot_f, axis=(0, 1)))
    conv_out = conv_sum.astype(jnp.bfloat16)
    kernel_grad = jnp.stack(kernel_rows)
    cot_pad = both_pad[1].astype(jnp.float32)
    back_sum = jnp.zeros((local_utts, frames_dev, width), jnp.float32)
    for offset in range(tap_count):
        begin = 2 * half_taps - offset
        back_sum = back_sum + kernel_f[offset] * cot_pad[:, begin : begin + frames_dev]
    hidden_grad = (back_sum * valid_rows[:, :, None]).astype(jnp.bfloat16)
    grad_flat = hidden_grad.reshape(local_utts * frames_dev, width)
    context_grad = lax.dot_general(
        grad_flat, out_weight, (((1,), (1,)), ((), ())), preferred_element_type=jnp.float32
    )
    context_grad = context_grad.reshape(local_utts, frames_dev, width).astype(jnp.bfloat16)
    weight_half, member = group_picks(context_flat, grad_flat, pick_weight, "dp", 1)
    kernel_vals = pick_entries(kernel_grad, pick_kernel)
    half_count = weight_half.shape[0]
    joined = butterfly_sum(jnp.concatenate([weight_half, kernel_vals]), ("dp", "seq"), {"dp": 2})
    dp_count = lax.axis_size("dp")
    other = lax.ppermute(joined, "dp", [(i, i ^ 1) for i in range(dp_count)])
    low, high = jnp.where(member == 0, joined, other), jnp.where(member == 0, other, joined)
    total = pick_weight.shape[0]
    weight_sum = jnp.concatenate([low[:half_count], high[:half_count]])[:total]
    kernel_sum = low[half_count:] + high[half_count:]
    total_slots = local_utts * lax.axis_size("dp") * full_frames
    norm_factor = 1.0 / math.sqrt(total_slots)
    return (conv_out, context_grad, weight_sum * norm_factor, kernel_sum * norm_factor)


def solution(mesh):
    placed = (
        P("dp", "seq", None),
        P("dp", "seq", None),
        P("dp", "seq", None),
        P("dp", "seq", None),
        P("dp"),
        P(),
        P(),
        P("dp", "seq", None),
        P(),
        P(),
    )
    return jax.shard_map(
        on_device,
        mesh=mesh,
        in_specs=placed,
        out_specs=(P("dp", "seq", None), P("dp", "seq", None), P(), P()),
        check_vma=False,
    )
```

```python
import math

import jax
import jax.numpy as jnp
from jax import lax
from jax.sharding import PartitionSpec as P

HEADS = 16


neg_big = -1e30


def padded(value, sides, width):
    for axis, dim in sides:
        count, length = (lax.axis_size(axis), value.shape[dim])
        up = [(i, (i + 1) % count) for i in range(count - 1)]
        down = [(j, i) for i, j in up]
        last = lax.slice_in_dim(value, length - width, length, axis=dim)
        leading = lax.slice_in_dim(value, 0, width, axis=dim)
        before = lax.ppermute(last, axis, up)
        after = lax.ppermute(leading, axis, down)
        value = jnp.concatenate([before, value, after], axis=dim)
    return value


def softmax_rows(scores, key_ok):
    scores = jnp.where(key_ok, scores, neg_big)
    row_max = jnp.max(scores, axis=-1, keepdims=True)
    probs = jnp.exp(scores - row_max)
    return (probs.astype(jnp.bfloat16), jnp.sum(probs, axis=-1))


def pick_entries(table, picks):
    flat = table.reshape(-1)
    lane = math.gcd(flat.shape[0], 128)
    blocks = flat.reshape(flat.shape[0] // lane, lane)
    chosen = jnp.take(blocks, picks // lane, axis=0)
    lane_ids = jnp.arange(lane, dtype=jnp.int32)
    hit = lane_ids[None, :] == (picks % lane)[:, None]
    return jnp.sum(jnp.where(hit, chosen, jnp.float32(0.0)), axis=1)

def block_entries(blocks, block_of, lane_of):
    chosen = jnp.take(blocks, block_of, axis=0)
    lane_ids = jnp.arange(blocks.shape[1], dtype=jnp.int32)
    hit = lane_ids[None, :] == lane_of[:, None]
    return jnp.sum(jnp.where(hit, chosen, jnp.float32(0.0)), axis=1)


def group_picks(context_flat, grad_flat, picks, axis, levels):
    count = lax.axis_size(axis)
    levels = min(levels, count.bit_length() - 1)
    group = 1 << levels
    pair = jnp.stack([context_flat, grad_flat])
    for level in range(levels):
        step = 1 << level
        other = lax.ppermute(pair, axis, [(i, i ^ step) for i in range(count)])
        pair = jnp.concatenate([pair, other], axis=1)
    depth, table_rows = pair.shape[1], pair.shape[2]
    lane = math.gcd(table_rows, 128)
    grad_blocks = pair[1].reshape(depth, table_rows // lane, lane)
    table = jnp.einsum("ncl,nr->crl", grad_blocks, pair[0], preferred_element_type=jnp.float32)
    total = picks.shape[0]
    rows = -(-total // group)
    padded_picks = jnp.pad(picks, (0, rows * group - total))
    first = (lax.axis_index(axis) % group) * rows
    mine = lax.dynamic_slice(padded_picks, (first,), (rows,))
    block_of = (mine % table_rows) // lane * table_rows + mine // table_rows
    values = block_entries(table.reshape(-1, lane), block_of, mine % lane)
    return values, lax.axis_index(axis) % group


def butterfly_sum(value, axes, first_step=None):
    first_step = first_step or {}
    for axis in axes:
        count = lax.axis_size(axis)
        step = first_step.get(axis, 1)
        while step < count:
            pairs = [(i, i ^ step) for i in range(count)]
            value = value + lax.ppermute(value, axis, pairs)
            step *= 2
    return value


def attend(query, key, value, key_ok, score_scale):
    scores = jnp.dot(query, key.T, preferred_element_type=jnp.float32) * score_scale
    weights, denom = softmax_rows(scores, key_ok[None, :])
    out_rows = jnp.dot(weights, value, preferred_element_type=jnp.float32)
    return (out_rows / denom[:, None]).astype(jnp.bfloat16)


def lane_dense_all_to_all(value):
    chunk = math.prod(value.shape[1:])
    if chunk % 128:
        return lax.all_to_all(value, "seq", 0, 0, tiled=True)
    dense = value.reshape(value.shape[0], chunk // 128, 128)
    return lax.all_to_all(dense, "seq", 0, 0, tiled=True).reshape(value.shape)


def head_attention(queries, key_rows, value_rows, utt_lengths, seq_index, score_scale, later):
    local_utts, frames_dev, width = queries.shape
    head_size = width // HEADS
    seq_count = HEADS * local_utts
    full_frames = frames_dev * seq_count
    stacked = jnp.stack([queries, key_rows, value_rows])
    stacked = stacked.reshape(3, local_utts, frames_dev, HEADS, head_size)
    stacked = stacked.transpose(3, 1, 0, 2, 4).reshape(seq_count, 3, frames_dev, head_size)
    gathered = lane_dense_all_to_all(stacked)
    gathered, later = lax.optimization_barrier((gathered, later))
    gathered = gathered.transpose(1, 0, 2, 3).reshape(3, full_frames, head_size)
    length = utt_lengths[seq_index % local_utts]
    key_ok = jnp.arange(full_frames, dtype=jnp.int32) < length
    out_rows = attend(gathered[0], gathered[1], gathered[2], key_ok, score_scale)
    out_rows = out_rows.reshape(seq_count, frames_dev, head_size)
    back = lane_dense_all_to_all(out_rows)
    back = back.reshape(HEADS, local_utts, frames_dev, head_size).transpose(1, 2, 0, 3)
    return back.reshape(local_utts, frames_dev, width), later


def frame_attention(queries, key_rows, value_rows, utt_lengths, score_scale):
    local_utts, frames_dev, width = queries.shape
    head_size = width // HEADS
    all_keys = lax.all_gather(key_rows, "seq", axis=1, tiled=True)
    all_values = lax.all_gather(value_rows, "seq", axis=1, tiled=True)
    full_frames = all_keys.shape[1]
    full_ids = jnp.arange(full_frames, dtype=jnp.int32)

    def one_utt(item):
        query_utt, key_utt, value_utt, length_utt = item
        query_heads = query_utt.reshape(frames_dev, HEADS, head_size)
        key_heads = key_utt.reshape(full_frames, HEADS, head_size)
        value_heads = value_utt.reshape(full_frames, HEADS, head_size)
        scores = (
            jnp.einsum("qhd,khd->hqk", query_heads, key_heads, preferred_element_type=jnp.float32)
            * score_scale
        )
        weights, denom = softmax_rows(scores, (full_ids < length_utt)[None, None, :])
        out_rows = jnp.einsum(
            "hqk,khd->qhd", weights, value_heads, preferred_element_type=jnp.float32
        )
        out_rows = out_rows / denom.transpose(1, 0)[:, :, None]
        return out_rows.astype(jnp.bfloat16).reshape(frames_dev, width)

    return lax.map(one_utt, (queries, all_keys, all_values, utt_lengths))


def on_device(
    queries,
    key_rows,
    value_rows,
    layer_input,
    utt_lengths,
    out_weight,
    conv_kernel,
    conv_cotangent,
    pick_weight,
    pick_kernel,
):
    local_utts, frames_dev, width = queries.shape
    seq_count = lax.axis_size("seq")
    full_frames = frames_dev * seq_count
    head_size = width // HEADS
    score_scale = 1.0 / math.sqrt(head_size)
    first_frame = lax.axis_index("seq") * frames_dev
    local_ids = first_frame + jnp.arange(frames_dev, dtype=jnp.int32)
    valid_rows = (local_ids[None, :] < utt_lengths[:, None]).astype(jnp.float32)
    seq_index = lax.axis_index("seq")
    if HEADS * local_utts == seq_count:
        context, conv_cotangent = head_attention(
            queries, key_rows, value_rows, utt_lengths, seq_index, score_scale, conv_cotangent
        )
    else:
        context = frame_attention(queries, key_rows, value_rows, utt_lengths, score_scale)
    context_flat = context.reshape(local_utts * frames_dev, width)
    projected = jnp.dot(context_flat, out_weight, preferred_element_type=jnp.float32).reshape(
        local_utts, frames_dev, width
    )
    hidden = ((layer_input.astype(jnp.float32) + projected) * valid_rows[:, :, None]).astype(
        jnp.bfloat16
    )
    tap_count = conv_kernel.shape[0]
    half_taps = (tap_count - 1) // 2
    kernel_f = conv_kernel.astype(jnp.float32)
    both_pad = padded(jnp.stack([hidden, conv_cotangent]), (("seq", 2),), half_taps)
    hidden_pad = both_pad[0]
    cot_f = conv_cotangent.astype(jnp.float32)
    conv_sum = jnp.zeros((local_utts, frames_dev, width), jnp.float32)
    kernel_rows = []
    for offset in range(tap_count):
        window = hidden_pad[:, offset : offset + frames_dev].astype(jnp.float32)
        conv_sum = conv_sum + kernel_f[offset] * window
        kernel_rows.append(jnp.sum(window * cot_f, axis=(0, 1)))
    conv_out = conv_sum.astype(jnp.bfloat16)
    kernel_grad = jnp.stack(kernel_rows)
    cot_pad = both_pad[1].astype(jnp.float32)
    back_sum = jnp.zeros((local_utts, frames_dev, width), jnp.float32)
    for offset in range(tap_count):
        begin = 2 * half_taps - offset
        back_sum = back_sum + kernel_f[offset] * cot_pad[:, begin : begin + frames_dev]
    hidden_grad = (back_sum * valid_rows[:, :, None]).astype(jnp.bfloat16)
    grad_flat = hidden_grad.reshape(local_utts * frames_dev, width)
    context_grad = lax.dot_general(
        grad_flat, out_weight, (((1,), (1,)), ((), ())), preferred_element_type=jnp.float32
    )
    context_grad = context_grad.reshape(local_utts, frames_dev, width).astype(jnp.bfloat16)
    weight_half, member = group_picks(context_flat, grad_flat, pick_weight, "dp", 1)
    kernel_vals = pick_entries(kernel_grad, pick_kernel)
    half_count = weight_half.shape[0]
    joined = butterfly_sum(jnp.concatenate([weight_half, kernel_vals]), ("seq", "dp"), {"dp": 2})
    dp_count = lax.axis_size("dp")
    other = lax.ppermute(joined, "dp", [(i, i ^ 1) for i in range(dp_count)])
    low, high = jnp.where(member == 0, joined, other), jnp.where(member == 0, other, joined)
    total = pick_weight.shape[0]
    weight_sum = jnp.concatenate([low[:half_count], high[:half_count]])[:total]
    kernel_sum = low[half_count:] + high[half_count:]
    total_slots = local_utts * lax.axis_size("dp") * full_frames
    norm_factor = 1.0 / math.sqrt(total_slots)
    return (conv_out, context_grad, weight_sum * norm_factor, kernel_sum * norm_factor)


def solution(mesh):
    placed = (
        P("dp", "seq", None),
        P("dp", "seq", None),
        P("dp", "seq", None),
        P("dp", "seq", None),
        P("dp"),
        P(),
        P(),
        P("dp", "seq", None),
        P(),
        P(),
    )
    return jax.shard_map(
        on_device,
        mesh=mesh,
        in_specs=placed,
        out_specs=(P("dp", "seq", None), P("dp", "seq", None), P(), P()),
        check_vma=False,
    )
```

```python
import math

import jax
import jax.numpy as jnp
from jax import lax
from jax.sharding import PartitionSpec as P

HEADS = 16


neg_big = -1e30


def padded(value, sides, width):
    for axis, dim in sides:
        count, length = (lax.axis_size(axis), value.shape[dim])
        up = [(i, (i + 1) % count) for i in range(count - 1)]
        down = [(j, i) for i, j in up]
        last = lax.slice_in_dim(value, length - width, length, axis=dim)
        leading = lax.slice_in_dim(value, 0, width, axis=dim)
        before = lax.ppermute(last, axis, up)
        after = lax.ppermute(leading, axis, down)
        value = jnp.concatenate([before, value, after], axis=dim)
    return value


def softmax_rows(scores, key_ok):
    scores = jnp.where(key_ok, scores, neg_big)
    row_max = jnp.max(scores, axis=-1, keepdims=True)
    probs = jnp.exp(scores - row_max)
    return (probs.astype(jnp.bfloat16), jnp.sum(probs, axis=-1))


def pick_entries(table, picks):
    flat = table.reshape(-1)
    lane = math.gcd(flat.shape[0], 128)
    blocks = flat.reshape(flat.shape[0] // lane, lane)
    chosen = jnp.take(blocks, picks // lane, axis=0)
    lane_ids = jnp.arange(lane, dtype=jnp.int32)
    hit = lane_ids[None, :] == (picks % lane)[:, None]
    return jnp.sum(jnp.where(hit, chosen, jnp.float32(0.0)), axis=1)

def block_entries(blocks, block_of, lane_of):
    chosen = jnp.take(blocks, block_of, axis=0)
    lane_ids = jnp.arange(blocks.shape[1], dtype=jnp.int32)
    hit = lane_ids[None, :] == lane_of[:, None]
    return jnp.sum(jnp.where(hit, chosen, jnp.float32(0.0)), axis=1)


def group_picks(context_flat, grad_flat, picks, axis, levels):
    count = lax.axis_size(axis)
    levels = min(levels, count.bit_length() - 1)
    group = 1 << levels
    pair = jnp.stack([context_flat, grad_flat])
    for level in range(levels):
        step = 1 << level
        other = lax.ppermute(pair, axis, [(i, i ^ step) for i in range(count)])
        pair = jnp.concatenate([pair, other], axis=1)
    depth, table_rows = pair.shape[1], pair.shape[2]
    lane = math.gcd(table_rows, 128)
    grad_blocks = pair[1].reshape(depth, table_rows // lane, lane)
    table = jnp.einsum("ncl,nr->crl", grad_blocks, pair[0], preferred_element_type=jnp.float32)
    total = picks.shape[0]
    rows = -(-total // group)
    padded_picks = jnp.pad(picks, (0, rows * group - total))
    first = (lax.axis_index(axis) % group) * rows
    mine = lax.dynamic_slice(padded_picks, (first,), (rows,))
    block_of = (mine % table_rows) // lane * table_rows + mine // table_rows
    values = block_entries(table.reshape(-1, lane), block_of, mine % lane)
    return values, lax.axis_index(axis) % group


def butterfly_sum(value, axes, first_step=None):
    first_step = first_step or {}
    for axis in axes:
        count = lax.axis_size(axis)
        step = first_step.get(axis, 1)
        while step < count:
            pairs = [(i, i ^ step) for i in range(count)]
            value = value + lax.ppermute(value, axis, pairs)
            step *= 2
    return value


def attend(query, key, value, key_ok, score_scale):
    scores = jnp.dot(query, key.T, preferred_element_type=jnp.float32) * score_scale
    weights, denom = softmax_rows(scores, key_ok[None, :])
    out_rows = jnp.dot(weights, value, preferred_element_type=jnp.float32)
    return (out_rows / denom[:, None]).astype(jnp.bfloat16)


def lane_dense_all_to_all(value):
    chunk = math.prod(value.shape[1:])
    if chunk % 128:
        return lax.all_to_all(value, "seq", 0, 0, tiled=True)
    dense = value.reshape(value.shape[0], chunk // 128, 128)
    return lax.all_to_all(dense, "seq", 0, 0, tiled=True).reshape(value.shape)


def head_attention(queries, key_rows, value_rows, utt_lengths, seq_index, score_scale, later):
    local_utts, frames_dev, width = queries.shape
    head_size = width // HEADS
    seq_count = HEADS * local_utts
    full_frames = frames_dev * seq_count
    stacked = jnp.stack([queries, key_rows, value_rows])
    stacked = stacked.reshape(3, local_utts, frames_dev, HEADS, head_size)
    stacked = stacked.transpose(3, 1, 0, 2, 4).reshape(seq_count, 3, frames_dev, head_size)
    gathered = lane_dense_all_to_all(stacked)
    later = later
    gathered = gathered.transpose(1, 0, 2, 3).reshape(3, full_frames, head_size)
    length = utt_lengths[seq_index % local_utts]
    key_ok = jnp.arange(full_frames, dtype=jnp.int32) < length
    out_rows = attend(gathered[0], gathered[1], gathered[2], key_ok, score_scale)
    out_rows = out_rows.reshape(seq_count, frames_dev, head_size)
    back = lane_dense_all_to_all(out_rows)
    back = back.reshape(HEADS, local_utts, frames_dev, head_size).transpose(1, 2, 0, 3)
    return back.reshape(local_utts, frames_dev, width), later


def frame_attention(queries, key_rows, value_rows, utt_lengths, score_scale):
    local_utts, frames_dev, width = queries.shape
    head_size = width // HEADS
    all_keys = lax.all_gather(key_rows, "seq", axis=1, tiled=True)
    all_values = lax.all_gather(value_rows, "seq", axis=1, tiled=True)
    full_frames = all_keys.shape[1]
    full_ids = jnp.arange(full_frames, dtype=jnp.int32)

    def one_utt(item):
        query_utt, key_utt, value_utt, length_utt = item
        query_heads = query_utt.reshape(frames_dev, HEADS, head_size)
        key_heads = key_utt.reshape(full_frames, HEADS, head_size)
        value_heads = value_utt.reshape(full_frames, HEADS, head_size)
        scores = (
            jnp.einsum("qhd,khd->hqk", query_heads, key_heads, preferred_element_type=jnp.float32)
            * score_scale
        )
        weights, denom = softmax_rows(scores, (full_ids < length_utt)[None, None, :])
        out_rows = jnp.einsum(
            "hqk,khd->qhd", weights, value_heads, preferred_element_type=jnp.float32
        )
        out_rows = out_rows / denom.transpose(1, 0)[:, :, None]
        return out_rows.astype(jnp.bfloat16).reshape(frames_dev, width)

    return lax.map(one_utt, (queries, all_keys, all_values, utt_lengths))


def on_device(
    queries,
    key_rows,
    value_rows,
    layer_input,
    utt_lengths,
    out_weight,
    conv_kernel,
    conv_cotangent,
    pick_weight,
    pick_kernel,
):
    local_utts, frames_dev, width = queries.shape
    seq_count = lax.axis_size("seq")
    full_frames = frames_dev * seq_count
    head_size = width // HEADS
    score_scale = 1.0 / math.sqrt(head_size)
    first_frame = lax.axis_index("seq") * frames_dev
    local_ids = first_frame + jnp.arange(frames_dev, dtype=jnp.int32)
    valid_rows = (local_ids[None, :] < utt_lengths[:, None]).astype(jnp.float32)
    seq_index = lax.axis_index("seq")
    if HEADS * local_utts == seq_count:
        context, conv_cotangent = head_attention(
            queries, key_rows, value_rows, utt_lengths, seq_index, score_scale, conv_cotangent
        )
    else:
        context = frame_attention(queries, key_rows, value_rows, utt_lengths, score_scale)
    context_flat = context.reshape(local_utts * frames_dev, width)
    projected = jnp.dot(context_flat, out_weight, preferred_element_type=jnp.float32).reshape(
        local_utts, frames_dev, width
    )
    hidden = ((layer_input.astype(jnp.float32) + projected) * valid_rows[:, :, None]).astype(
        jnp.bfloat16
    )
    tap_count = conv_kernel.shape[0]
    half_taps = (tap_count - 1) // 2
    kernel_f = conv_kernel.astype(jnp.float32)
    both_pad = padded(jnp.stack([hidden, conv_cotangent]), (("seq", 2),), half_taps)
    hidden_pad = both_pad[0]
    cot_f = conv_cotangent.astype(jnp.float32)
    conv_sum = jnp.zeros((local_utts, frames_dev, width), jnp.float32)
    kernel_rows = []
    for offset in range(tap_count):
        window = hidden_pad[:, offset : offset + frames_dev].astype(jnp.float32)
        conv_sum = conv_sum + kernel_f[offset] * window
        kernel_rows.append(jnp.sum(window * cot_f, axis=(0, 1)))
    conv_out = conv_sum.astype(jnp.bfloat16)
    kernel_grad = jnp.stack(kernel_rows)
    cot_pad = both_pad[1].astype(jnp.float32)
    back_sum = jnp.zeros((local_utts, frames_dev, width), jnp.float32)
    for offset in range(tap_count):
        begin = 2 * half_taps - offset
        back_sum = back_sum + kernel_f[offset] * cot_pad[:, begin : begin + frames_dev]
    hidden_grad = (back_sum * valid_rows[:, :, None]).astype(jnp.bfloat16)
    grad_flat = hidden_grad.reshape(local_utts * frames_dev, width)
    context_grad = lax.dot_general(
        grad_flat, out_weight, (((1,), (1,)), ((), ())), preferred_element_type=jnp.float32
    )
    context_grad = context_grad.reshape(local_utts, frames_dev, width).astype(jnp.bfloat16)
    weight_half, member = group_picks(context_flat, grad_flat, pick_weight, "dp", 1)
    kernel_vals = pick_entries(kernel_grad, pick_kernel)
    half_count = weight_half.shape[0]
    joined = butterfly_sum(jnp.concatenate([weight_half, kernel_vals]), ("dp", "seq"), {"dp": 2})
    dp_count = lax.axis_size("dp")
    other = lax.ppermute(joined, "dp", [(i, i ^ 1) for i in range(dp_count)])
    low, high = jnp.where(member == 0, joined, other), jnp.where(member == 0, other, joined)
    total = pick_weight.shape[0]
    weight_sum = jnp.concatenate([low[:half_count], high[:half_count]])[:total]
    kernel_sum = low[half_count:] + high[half_count:]
    total_slots = local_utts * lax.axis_size("dp") * full_frames
    norm_factor = 1.0 / math.sqrt(total_slots)
    return (conv_out, context_grad, weight_sum * norm_factor, kernel_sum * norm_factor)


def solution(mesh):
    placed = (
        P("dp", "seq", None),
        P("dp", "seq", None),
        P("dp", "seq", None),
        P("dp", "seq", None),
        P("dp"),
        P(),
        P(),
        P("dp", "seq", None),
        P(),
        P(),
    )
    return jax.shard_map(
        on_device,
        mesh=mesh,
        in_specs=placed,
        out_specs=(P("dp", "seq", None), P("dp", "seq", None), P(), P()),
        check_vma=False,
    )
```
